128 devices in a mesh: dp: 32 (over x, z_hi, y), tensor: 4 (over z_lo, core).
Axes of the slice: x: 4, y: 4, z: 4 (z_hi: 2, z_lo: 2; z = z_hi * 2 + z_lo), core: 2. Of those that a mesh axis runs over, the one named last changes fastest.
Arguments:
- tokens: bfloat16 [65536, 1024], P(('dp', 'tensor')), may hold values from -16 to 16
- prompts: bfloat16 [32, 64, 1024], P('dp'), may hold values from -6 to 6
- w_attn: bfloat16 [3, 1024, 1024], P(None, None, 'tensor'), may hold values from -0.1875 to 0.1875
- w_out: bfloat16 [1024, 1024], P('tensor'), may hold values from -0.1875 to 0.1875
- norm_gain: float32 [2, 1024], replicated, may hold values from 0.1 to 1.9
- norm_bias: float32 [2, 1024], replicated, may hold values from -3 to 3
- w_in: bfloat16 [1024, 4096], P(None, 'tensor'), may hold values from -0.1875 to 0.1875
- b_in: float32 [4096], P('tensor'), may hold values from -3 to 3
- w_down: bfloat16 [4096, 1024], P('tensor'), may hold values from -0.09375 to 0.09375
- index_rows: bfloat16 [65536, 1024], P('dp'), may hold values from -6 to 6
- lengths: int32 [32, 32], P('dp'), may hold values from 1 to 512, 2048 in all within a row
- groups: int32 [1024], P('dp'), may hold values from 0 to 31
- candidates: int32 [1024, 64], P(('dp', 'tensor')), may hold values from 0 to 65535
Outputs:
- scores: float32 [1024, 64], P(('dp', 'tensor'))
The draws below stay inside these ranges and needn't reach their ends.
All inputs are finite; a program needn't handle non-finite values.
Results may differ from the reference program's by a relative error of at most 0.01.
Values may be sent and summed in bfloat16 or wider, within the bound.
No kernel may reach another device: no remote copies, remote signals or barrier semaphores. Data moves between devices by JAX's collectives and lax.ppermute only.
A program may use at most 128 MiB of HBM per device.

```python
import math
import jax
import jax.numpy as jnp
import numpy as np
from jax import lax

D = 1024
HEADS = 16
FF = 4096
HEAD_DIM = 64
TOK_DEV = 2048
TEXTS_DEV = 32
MAXLEN = 512
PLEN = 64
CANDS = 64
TOKENS = 65536
TEXTS = 1024
GROUPS = 32
INDEX = 65536
N_DP = 32


def draw_tokens(key, part):
    first = jax.random.fold_in(jax.random.fold_in(key, 11), 0)
    base = jnp.clip(jax.random.normal(first, (TOKENS, D), jnp.float32), -6.0, 6.0)
    return base.astype(jnp.bfloat16)


def plant(entries, stream_key, least, high):
    place = [jax.random.randint(jax.random.fold_in(stream_key, axis), (), 0, length) for axis, length in enumerate(entries.shape)]
    main_axis = entries.shape.index(max(entries.shape))
    beside = place[:main_axis] + [(place[main_axis] + 1) % entries.shape[main_axis]] + place[main_axis + 1:]
    return entries.at[tuple(place)].set(least).at[tuple(beside)].set(high)


def block_levels(rng, extent, pieces, low, top_value):
    def one(dim, blocks):
        heights = jax.random.uniform(jax.random.fold_in(jax.random.fold_in(rng, 6), dim), (blocks,), jnp.float32, low / len(pieces), top_value / len(pieces))
        return jnp.repeat(jnp.exp(heights), extent[dim] // blocks).reshape((-1,) + (1,) * (len(extent) - dim - 1))

    loudness = one(*pieces[0])
    for cut in pieces[1:]:
        loudness = loudness * one(*cut)
    return loudness


def rank_table(amount, slope):
    loads = [(1 << 20) // math.isqrt(standing ** slope) + 1 for standing in range(1, amount + 1)]
    deviation = 1 + sum(loads) // (1 << 30)
    return np.cumsum(np.array([max(1, weight // deviation) for weight in loads]))


def ranked(own_key, shape, number_of, lean):
    table = rank_table(number_of, lean)
    lot = jax.random.randint(jax.random.fold_in(own_key, 1), shape, 0, int(table[number_of - 1]))
    rank = jnp.searchsorted(jnp.asarray(table, jnp.int32), lot, side="right")
    return jax.random.permutation(jax.random.fold_in(own_key, 2), number_of)[rank].astype(jnp.int32)


def length_profile(amount, total, most, slope):
    weights = [(1 << 20) // math.isqrt(grade ** slope) + 1 for grade in range(2, amount + 1)]
    spare, given = total - most - (amount - 1), [1] * (amount - 1)
    while spare > 0:
        free = [i for i in range(amount - 1) if given[i] < most]
        mass, budget = sum([weights[i] for i in free]), spare
        for i in free:
            extra = min(most - given[i], max(1, budget * weights[i] // mass), spare)
            given[i] = given[i] + extra
            spare = spare - extra
    return np.array([most] + given)


def uneven(key, number_of, total, limit, slope):
    if number_of == 2:
        one = jax.random.randint(key, (), max(1, total - limit), min(limit, total - 1) + 1)
        return jnp.stack([one, total - one])
    sizes = jnp.asarray(length_profile(number_of, total, limit, slope), jnp.int32)
    pairs = (number_of - 1) // 2
    source_of, sink = sizes[1:1 + 2 * pairs:2], sizes[2:2 + 2 * pairs:2]
    room = jnp.minimum(source_of - 1, limit - sink)
    passed = jax.random.randint(jax.random.fold_in(key, 1), (pairs,), 0, 1 << 20) % (room + 1)
    sizes = sizes.at[1:1 + 2 * pairs:2].set(source_of - passed).at[2:2 + 2 * pairs:2].set(sink + passed)
    return sizes[jax.random.permutation(jax.random.fold_in(key, 2), number_of)]


def bell_draw(stream_key, extent, spread, most, shards=(), held_as=jnp.bfloat16):
    loudness = block_levels(stream_key, extent, shards, -0.22, 0.18) if shards else 1.0
    values = jax.random.normal(stream_key, extent, jnp.float32) * spread * loudness
    return jnp.minimum(jnp.maximum(values, -most), most).astype(held_as)


def setup_inputs(seed: int = 0) -> dict:
    arg_keys = jax.random.split(jax.random.key(seed), 14)
    return {
        "tokens": draw_tokens(jax.random.fold_in(arg_keys[13], 71), 0),
        "prompts": bell_draw(arg_keys[1], (GROUPS, PLEN, D), 1.0, 6.0, ((0, 32),)),
        "w_attn": bell_draw(arg_keys[2], (3, D, D), D ** -0.5, 0.1875, ((2, 4),)),
        "w_out": bell_draw(arg_keys[3], (D, D), D ** -0.5, 0.1875, ((0, 4),)),
        "norm_gain": jnp.clip(1.0 + 0.18 * jax.random.normal(arg_keys[4], (2, D), jnp.float32), 0.1, 1.9),
        "norm_bias": bell_draw(arg_keys[5], (2, D), 0.5, 3.0, (), jnp.float32),
        "w_in": bell_draw(arg_keys[6], (D, FF), D ** -0.5, 0.1875, ((1, 4),)),
        "b_in": bell_draw(arg_keys[7], (FF,), 0.5, 3.0, ((0, 4),), jnp.float32),
        "w_down": bell_draw(arg_keys[8], (FF, D), FF ** -0.5, 0.09375, ((0, 4),)),
        "index_rows": bell_draw(arg_keys[9], (INDEX, D), 1.0, 6.0, ((0, 32),)),
        "lengths": jax.vmap(lambda own: uneven(own, TEXTS_DEV, TOK_DEV, MAXLEN, 2))(jax.random.split(arg_keys[10], N_DP)).reshape((N_DP, TEXTS_DEV)).astype(jnp.int32),
        "groups": plant(ranked(arg_keys[11], (TEXTS,), GROUPS, 1), jax.random.fold_in(arg_keys[11], 3), 0, GROUPS - 1).astype(jnp.int32),
        "candidates": plant(jax.random.randint(arg_keys[12], (TEXTS, CANDS), 0, INDEX), jax.random.fold_in(arg_keys[12], 1), 0, INDEX - 1).astype(jnp.int32),
    }


def layer_norm(values, gain, bias):
    mean = lax.optimization_barrier(jnp.mean(values, axis=-1, keepdims=True))
    centred = values - mean
    var = lax.optimization_barrier(jnp.mean(centred * centred, axis=-1, keepdims=True))
    return centred * lax.rsqrt(var + 1e-05) * gain + bias

def reference(tokens, prompts, w_attn, w_out, norm_gain, norm_bias, w_in, b_in, w_down, index_rows, lengths, groups, candidates):
    scale = HEAD_DIM ** (-0.5)
    flat_prompts = prompts.reshape(GROUPS * PLEN, D)
    prompt_key = jnp.dot(flat_prompts, w_attn[1], preferred_element_type=jnp.float32).astype(jnp.bfloat16)
    prompt_value = jnp.dot(flat_prompts, w_attn[2], preferred_element_type=jnp.float32).astype(jnp.bfloat16)
    key_group = jnp.arange(GROUPS * PLEN, dtype=jnp.int32) // PLEN
    text_ids = jnp.arange(TEXTS_DEV, dtype=jnp.int32)

    def one_pack(packed):
        block, lens, grp = packed
        ends = jnp.cumsum(lens).astype(jnp.int32)
        position = jnp.arange(TOK_DEV, dtype=jnp.int32)
        seg = lax.optimization_barrier(jnp.sum((position[:, None] >= ends[None, :]).astype(jnp.int32), axis=1)).astype(jnp.int32)
        same_text = seg[:, None] == text_ids[None, :]
        tok_group = lax.optimization_barrier(jnp.sum(jnp.where(same_text, grp[None, :], 0), axis=1)).astype(jnp.int32)
        query = (jnp.dot(block, w_attn[0], preferred_element_type=jnp.float32) * scale).astype(jnp.bfloat16)
        keys = jnp.dot(block, w_attn[1], preferred_element_type=jnp.float32).astype(jnp.bfloat16)
        values = jnp.dot(block, w_attn[2], preferred_element_type=jnp.float32).astype(jnp.bfloat16)
        allowed = jnp.concatenate([seg[:, None] == seg[None, :], tok_group[:, None] == key_group[None, :]], axis=1)

        def one_head(head):
            start = head * HEAD_DIM
            q_head = lax.dynamic_slice_in_dim(query, start, HEAD_DIM, 1)
            k_head = jnp.concatenate([lax.dynamic_slice_in_dim(keys, start, HEAD_DIM, 1), lax.dynamic_slice_in_dim(prompt_key, start, HEAD_DIM, 1)], axis=0)
            v_head = jnp.concatenate([lax.dynamic_slice_in_dim(values, start, HEAD_DIM, 1), lax.dynamic_slice_in_dim(prompt_value, start, HEAD_DIM, 1)], axis=0)
            logits = jnp.dot(q_head, k_head.T, preferred_element_type=jnp.float32)
            logits = jnp.where(allowed, logits, jnp.float32(-1e+30))
            top = lax.optimization_barrier(jnp.max(logits, axis=1, keepdims=True))
            weights = jnp.exp(logits - top)
            total = lax.optimization_barrier(jnp.sum(weights, axis=1, keepdims=True))
            probs = (weights / total).astype(jnp.bfloat16)
            return jnp.dot(probs, v_head, preferred_element_type=jnp.float32).astype(jnp.bfloat16)
        context = lax.map(one_head, jnp.arange(HEADS, dtype=jnp.int32))
        context = jnp.transpose(context, (1, 0, 2)).reshape(TOK_DEV, D)
        attended = jnp.dot(context, w_out, preferred_element_type=jnp.float32)
        normed = layer_norm(block.astype(jnp.float32) + attended, norm_gain[0], norm_bias[0]).astype(jnp.bfloat16)
        expanded = jax.nn.gelu(jnp.dot(normed, w_in, preferred_element_type=jnp.float32) + b_in, approximate=False).astype(jnp.bfloat16)
        reduced = jnp.dot(expanded, w_down, preferred_element_type=jnp.float32)
        output = layer_norm(normed.astype(jnp.float32) + reduced, norm_gain[1], norm_bias[1]).astype(jnp.bfloat16)
        member = (text_ids[:, None] == seg[None, :]).astype(jnp.bfloat16)
        sums = jnp.dot(member, output, preferred_element_type=jnp.float32)
        pooled = sums / lens[:, None].astype(jnp.float32)
        square = lax.optimization_barrier(jnp.mean(pooled * pooled, axis=1, keepdims=True))
        return (pooled * lax.rsqrt(square + 1e-06)).astype(jnp.bfloat16)
    embedded = lax.map(one_pack, (tokens.reshape(N_DP, TOK_DEV, D), lengths, groups.reshape(N_DP, TEXTS_DEV)))
    embedded = embedded.reshape(TEXTS, D)

    def one_text(pair):
        vector, chosen = pair
        rows = jnp.take(index_rows, chosen, axis=0)
        return jnp.dot(rows, vector, preferred_element_type=jnp.float32) * D ** (-0.5)
    return lax.map(one_text, (embedded, candidates))
```

```python
import jax
import jax.numpy as jnp
from jax import lax
from jax.sharding import PartitionSpec as P

D = 1024
HEAD_DIM = 64


def layer_norm(values, gain, bias):
    mean = jnp.mean(values, axis=-1, keepdims=True)
    centred = values - mean
    var = jnp.mean(centred * centred, axis=-1, keepdims=True)
    return centred * lax.rsqrt(var + 1e-05) * gain + bias


def project(block, weight):
    return jnp.dot(block, weight, preferred_element_type=jnp.float32).astype(jnp.bfloat16)


def shards(
    tokens,
    prompts,
    w_attn,
    w_out,
    norm_gain,
    norm_bias,
    w_in,
    b_in,
    w_down,
    index_rows,
    lengths,
    groups,
    candidates,
):
    shard_rows = tokens.shape[0]
    tok_dev = shard_rows * lax.axis_size("tensor")
    columns = w_attn.shape[2]
    heads_here = columns // HEAD_DIM
    scale = HEAD_DIM ** (-0.5)
    whole = lax.all_gather(tokens, "tensor", axis=0, tiled=True)
    query = (jnp.dot(whole, w_attn[0], preferred_element_type=jnp.float32) * scale).astype(
        jnp.bfloat16
    )
    keys = project(whole, w_attn[1])
    values = project(whole, w_attn[2])
    every_prompt = lax.all_gather(prompts, "dp", axis=0, tiled=True)
    flat = every_prompt.reshape(-1, every_prompt.shape[2])
    prompt_key = project(flat, w_attn[1])
    prompt_value = project(flat, w_attn[2])
    prompt_len = prompts.shape[1]
    prompt_rows = prompt_key.shape[0]
    lens = lengths[0]
    texts_here = lens.shape[0]
    text_ids = jnp.arange(texts_here, dtype=jnp.int32)
    ends = jnp.cumsum(lens)
    position = jnp.arange(tok_dev, dtype=jnp.int32)
    seg = jnp.sum((position[:, None] >= ends[None, :]).astype(jnp.int32), axis=1)
    tok_group = jnp.sum(jnp.where(seg[:, None] == text_ids[None, :], groups[None, :], 0), axis=1)
    key_group = jnp.arange(prompt_rows, dtype=jnp.int32) // prompt_len
    all_keys = jnp.concatenate([keys, prompt_key], axis=0).reshape(-1, heads_here, HEAD_DIM)
    all_values = jnp.concatenate([values, prompt_value], axis=0).reshape(-1, heads_here, HEAD_DIM)
    block = min(512, tok_dev)

    def attend(number):
        start = number * block
        q_block = lax.dynamic_slice_in_dim(query, start, block, 0).reshape(
            block, heads_here, HEAD_DIM
        )
        seg_block = lax.dynamic_slice_in_dim(seg, start, block, 0)
        group_block = lax.dynamic_slice_in_dim(tok_group, start, block, 0)
        allowed = jnp.concatenate(
            [seg_block[:, None] == seg[None, :], group_block[:, None] == key_group[None, :]], axis=1
        )
        logits = jnp.einsum("qhe,khe->hqk", q_block, all_keys, preferred_element_type=jnp.float32)
        logits = jnp.where(allowed[None], logits, jnp.float32(-1e30))
        top = jnp.max(logits, axis=2, keepdims=True)
        weights = jnp.exp(logits - top)
        total = jnp.sum(weights, axis=2, keepdims=True)
        probs = (weights / total).astype(jnp.bfloat16)
        mixed = jnp.einsum("hqk,khe->qhe", probs, all_values, preferred_element_type=jnp.float32)
        return mixed.astype(jnp.bfloat16).reshape(block, columns)

    context = lax.map(attend, jnp.arange(tok_dev // block, dtype=jnp.int32)).reshape(
        tok_dev, columns
    )
    my_start = lax.axis_index("tensor") * shard_rows
    attn_part = lax.psum_scatter(
        jnp.dot(context, w_out, preferred_element_type=jnp.float32),
        "tensor",
        scatter_dimension=0,
        tiled=True,
    )
    normed_rows = layer_norm(
        tokens.astype(jnp.float32) + attn_part, norm_gain[0], norm_bias[0]
    ).astype(jnp.bfloat16)
    expanded = jax.nn.gelu(
        jnp.dot(
            lax.all_gather(normed_rows, "tensor", axis=0, tiled=True),
            w_in,
            preferred_element_type=jnp.float32,
        )
        + b_in,
        approximate=False,
    ).astype(jnp.bfloat16)
    reduced = lax.psum_scatter(
        jnp.dot(expanded, w_down, preferred_element_type=jnp.float32).astype(jnp.bfloat16),
        "tensor",
        scatter_dimension=0,
        tiled=True,
    ).astype(jnp.float32)
    output = layer_norm(
        normed_rows.astype(jnp.float32) + reduced, norm_gain[1], norm_bias[1]
    ).astype(jnp.bfloat16)
    seg_rows = lax.dynamic_slice_in_dim(seg, my_start, shard_rows, 0)
    member = (text_ids[:, None] == seg_rows[None, :]).astype(jnp.bfloat16)
    partial_sums = jnp.dot(member, output, preferred_element_type=jnp.float32)
    pooled_sums = lax.psum_scatter(partial_sums, "tensor", scatter_dimension=0, tiled=True)
    mine = pooled_sums.shape[0]
    my_lens = lax.dynamic_slice_in_dim(lens, lax.axis_index("tensor") * mine, mine, 0)
    pooled = pooled_sums / my_lens[:, None].astype(jnp.float32)
    square = jnp.mean(pooled * pooled, axis=1, keepdims=True)
    embedding = (pooled * lax.rsqrt(square + 1e-06)).astype(jnp.bfloat16)
    n_dp = lax.axis_size("dp")
    asked_vectors = lax.all_to_all(
        jnp.broadcast_to(embedding[None], (n_dp,) + embedding.shape), "dp", 0, 0, tiled=True
    ).reshape(-1, embedding.shape[1])
    asked_rows = lax.all_to_all(
        jnp.broadcast_to(candidates[None], (n_dp,) + candidates.shape), "dp", 0, 0, tiled=True
    ).reshape(-1, candidates.shape[1])
    held = index_rows.shape[0]
    local_rows = asked_rows - lax.axis_index("dp") * held
    table = jnp.dot(asked_vectors, index_rows.T, preferred_element_type=jnp.float32) * D ** (-0.5)
    row_ids = jnp.arange(held, dtype=jnp.int32)
    picked = jnp.sum(
        jnp.where(local_rows[:, :, None] == row_ids[None, None, :], table[:, None, :], jnp.float32(0.0)),
        axis=2,
    )
    returned = lax.all_to_all(picked, "dp", 0, 0, tiled=True)
    return jnp.sum(returned.reshape(n_dp, -1, returned.shape[1]), axis=0)


def solution(mesh):
    placed = (
        P(("dp", "tensor"), None),
        P("dp", None, None),
        P(None, None, "tensor"),
        P("tensor", None),
        P(),
        P(),
        P(None, "tensor"),
        P("tensor"),
        P("tensor", None),
        P("dp", None),
        P("dp", None),
        P("dp"),
        P(("dp", "tensor"), None),
    )
    return jax.shard_map(
        shards, mesh=mesh, in_specs=placed, out_specs=P(("dp", "tensor"), None), check_vma=False
    )
```

```python
import jax
import jax.numpy as jnp
from jax import lax
from jax.sharding import PartitionSpec as P

D = 1024
HEAD_DIM = 64


def layer_norm(values, gain, bias):
    mean = jnp.mean(values, axis=-1, keepdims=True)
    centred = values - mean
    var = jnp.mean(centred * centred, axis=-1, keepdims=True)
    return centred * lax.rsqrt(var + 1e-05) * gain + bias


def project(block, weight):
    return jnp.dot(block, weight, preferred_element_type=jnp.float32).astype(jnp.bfloat16)


def shards(
    tokens,
    prompts,
    w_attn,
    w_out,
    norm_gain,
    norm_bias,
    w_in,
    b_in,
    w_down,
    index_rows,
    lengths,
    groups,
    candidates,
):
    shard_rows = tokens.shape[0]
    tok_dev = shard_rows * lax.axis_size("tensor")
    columns = w_attn.shape[2]
    heads_here = columns // HEAD_DIM
    scale = HEAD_DIM ** (-0.5)
    whole = lax.all_gather(tokens, "tensor", axis=0, tiled=True)
    query = (jnp.dot(whole, w_attn[0], preferred_element_type=jnp.float32) * scale).astype(
        jnp.bfloat16
    )
    keys = project(whole, w_attn[1])
    values = project(whole, w_attn[2])
    n_dp = lax.axis_size("dp")
    own_prompt = prompts.reshape(-1, prompts.shape[2])
    own_kv = jnp.concatenate([project(own_prompt, w_attn[1]), project(own_prompt, w_attn[2])], axis=1)
    every_kv = lax.all_to_all(
        jnp.broadcast_to(own_kv[None], (n_dp,) + own_kv.shape), "dp", 0, 0, tiled=True
    ).reshape(-1, 2 * columns)
    prompt_key = every_kv[:, :columns]
    prompt_value = every_kv[:, columns:]
    prompt_len = prompts.shape[1]
    prompt_rows = prompt_key.shape[0]
    lens = lengths[0]
    texts_here = lens.shape[0]
    text_ids = jnp.arange(texts_here, dtype=jnp.int32)
    ends = jnp.cumsum(lens)
    position = jnp.arange(tok_dev, dtype=jnp.int32)
    seg = jnp.sum((position[:, None] >= ends[None, :]).astype(jnp.int32), axis=1)
    tok_group = jnp.sum(jnp.where(seg[:, None] == text_ids[None, :], groups[None, :], 0), axis=1)
    key_group = jnp.arange(prompt_rows, dtype=jnp.int32) // prompt_len
    all_keys = jnp.concatenate([keys, prompt_key], axis=0).reshape(-1, heads_here, HEAD_DIM)
    all_values = jnp.concatenate([values, prompt_value], axis=0).reshape(-1, heads_here, HEAD_DIM)
    block = min(512, tok_dev)

    def attend(number):
        start = number * block
        q_block = lax.dynamic_slice_in_dim(query, start, block, 0).reshape(
            block, heads_here, HEAD_DIM
        )
        seg_block = lax.dynamic_slice_in_dim(seg, start, block, 0)
        group_block = lax.dynamic_slice_in_dim(tok_group, start, block, 0)
        allowed = jnp.concatenate(
            [seg_block[:, None] == seg[None, :], group_block[:, None] == key_group[None, :]], axis=1
        )
        logits = jnp.einsum("qhe,khe->hqk", q_block, all_keys, preferred_element_type=jnp.float32)
        logits = jnp.where(allowed[None], logits, jnp.float32(-1e30))
        top = jnp.max(logits, axis=2, keepdims=True)
        weights = jnp.exp(logits - top)
        total = jnp.sum(weights, axis=2, keepdims=True)
        probs = (weights / total).astype(jnp.bfloat16)
        mixed = jnp.einsum("hqk,khe->qhe", probs, all_values, preferred_element_type=jnp.float32)
        return mixed.astype(jnp.bfloat16).reshape(block, columns)

    context = lax.map(attend, jnp.arange(tok_dev // block, dtype=jnp.int32)).reshape(
        tok_dev, columns
    )
    my_start = lax.axis_index("tensor") * shard_rows
    attn_part = lax.psum_scatter(
        jnp.dot(context, w_out, preferred_element_type=jnp.float32).astype(jnp.bfloat16),
        "tensor",
        scatter_dimension=0,
        tiled=True,
    ).astype(jnp.float32)
    normed_rows = layer_norm(
        tokens.astype(jnp.float32) + attn_part, norm_gain[0], norm_bias[0]
    ).astype(jnp.bfloat16)
    expanded = jax.nn.gelu(
        jnp.dot(
            lax.all_gather(normed_rows, "tensor", axis=0, tiled=True),
            w_in,
            preferred_element_type=jnp.float32,
        )
        + b_in,
        approximate=False,
    ).astype(jnp.bfloat16)
    reduced = lax.psum_scatter(
        jnp.dot(expanded, w_down, preferred_element_type=jnp.float32).astype(jnp.bfloat16),
        "tensor",
        scatter_dimension=0,
        tiled=True,
    ).astype(jnp.float32)
    output = layer_norm(
        normed_rows.astype(jnp.float32) + reduced, norm_gain[1], norm_bias[1]
    ).astype(jnp.bfloat16)
    seg_rows = lax.dynamic_slice_in_dim(seg, my_start, shard_rows, 0)
    member = (text_ids[:, None] == seg_rows[None, :]).astype(jnp.bfloat16)
    partial_sums = jnp.dot(member, output, preferred_element_type=jnp.float32)
    pooled_sums = lax.psum_scatter(partial_sums, "tensor", scatter_dimension=0, tiled=True)
    mine = pooled_sums.shape[0]
    my_lens = lax.dynamic_slice_in_dim(lens, lax.axis_index("tensor") * mine, mine, 0)
    pooled = pooled_sums / my_lens[:, None].astype(jnp.float32)
    square = jnp.mean(pooled * pooled, axis=1, keepdims=True)
    embedding = (pooled * lax.rsqrt(square + 1e-06)).astype(jnp.bfloat16)
    asked_vectors = lax.all_to_all(
        jnp.broadcast_to(embedding[None], (n_dp,) + embedding.shape), "dp", 0, 0, tiled=True
    ).reshape(-1, embedding.shape[1])
    asked_rows = lax.all_to_all(
        jnp.broadcast_to(candidates[None], (n_dp,) + candidates.shape), "dp", 0, 0, tiled=True
    ).reshape(-1, candidates.shape[1])
    held = index_rows.shape[0]
    local_rows = asked_rows - lax.axis_index("dp") * held
    table = jnp.dot(asked_vectors, index_rows.T, preferred_element_type=jnp.float32) * D ** (-0.5)
    row_ids = jnp.arange(held, dtype=jnp.int32)
    picked = jnp.sum(
        jnp.where(local_rows[:, :, None] == row_ids[None, None, :], table[:, None, :], jnp.float32(0.0)),
        axis=2,
    )
    returned = lax.all_to_all(picked, "dp", 0, 0, tiled=True)
    return jnp.sum(returned.reshape(n_dp, -1, returned.shape[1]), axis=0)


def solution(mesh):
    placed = (
        P(("dp", "tensor"), None),
        P("dp", None, None),
        P(None, None, "tensor"),
        P("tensor", None),
        P(),
        P(),
        P(None, "tensor"),
        P("tensor"),
        P("tensor", None),
        P("dp", None),
        P("dp", None),
        P("dp"),
        P(("dp", "tensor"), None),
    )
    return jax.shard_map(
        shards, mesh=mesh, in_specs=placed, out_specs=P(("dp", "tensor"), None), check_vma=False
    )
```

```python
import jax
import jax.numpy as jnp
from jax import lax
from jax.sharding import PartitionSpec as P

D = 1024
HEAD_DIM = 64


def layer_norm(values, gain, bias):
    mean = jnp.mean(values, axis=-1, keepdims=True)
    centred = values - mean
    var = jnp.mean(centred * centred, axis=-1, keepdims=True)
    return centred * lax.rsqrt(var + 1e-05) * gain + bias


def project(block, weight):
    return jnp.dot(block, weight, preferred_element_type=jnp.float32).astype(jnp.bfloat16)


def shards(
    tokens,
    prompts,
    w_attn,
    w_out,
    norm_gain,
    norm_bias,
    w_in,
    b_in,
    w_down,
    index_rows,
    lengths,
    groups,
    candidates,
):
    shard_rows = tokens.shape[0]
    tok_dev = shard_rows * lax.axis_size("tensor")
    columns = w_attn.shape[2]
    heads_here = columns // HEAD_DIM
    scale = HEAD_DIM ** (-0.5)
    whole = lax.all_gather(tokens, "tensor", axis=0, tiled=True)
    query = (jnp.dot(whole, w_attn[0], preferred_element_type=jnp.float32) * scale).astype(
        jnp.bfloat16
    )
    keys = project(whole, w_attn[1])
    values = project(whole, w_attn[2])
    n_dp = lax.axis_size("dp")
    own_prompt = prompts.reshape(-1, prompts.shape[2])
    own_kv = jnp.concatenate([project(own_prompt, w_attn[1]), project(own_prompt, w_attn[2])], axis=1)
    every_kv = lax.all_to_all(
        jnp.broadcast_to(own_kv[None], (n_dp,) + own_kv.shape), "dp", 0, 0, tiled=True
    ).reshape(-1, 2 * columns)
    prompt_key = every_kv[:, :columns]
    prompt_value = every_kv[:, columns:]
    prompt_len = prompts.shape[1]
    prompt_rows = prompt_key.shape[0]
    lens = lengths[0]
    texts_here = lens.shape[0]
    text_ids = jnp.arange(texts_here, dtype=jnp.int32)
    ends = jnp.cumsum(lens)
    position = jnp.arange(tok_dev, dtype=jnp.int32)
    seg = jnp.sum((position[:, None] >= ends[None, :]).astype(jnp.int32), axis=1)
    tok_group = jnp.sum(jnp.where(seg[:, None] == text_ids[None, :], groups[None, :], 0), axis=1)
    groups_all = prompt_rows // prompt_len
    group_ids = jnp.arange(groups_all, dtype=jnp.int32)
    starts = ends - lens
    prompt_k4 = prompt_key.reshape(groups_all, prompt_len, heads_here, HEAD_DIM)
    prompt_v4 = prompt_value.reshape(groups_all, prompt_len, heads_here, HEAD_DIM)
    block = min(256, tok_dev)
    window = min(tok_dev, -(-(block + 2 * (512 - 1)) // 128) * 128)

    def attend(number):
        start = number * block
        q_block = lax.dynamic_slice_in_dim(query, start, block, 0).reshape(
            block, heads_here, HEAD_DIM
        )
        seg_block = lax.dynamic_slice_in_dim(seg, start, block, 0)
        group_block = lax.dynamic_slice_in_dim(tok_group, start, block, 0)
        first = jnp.clip(starts[seg_block[0]], 0, tok_dev - window)
        k_win = lax.dynamic_slice_in_dim(keys, first, window, 0).reshape(window, heads_here, HEAD_DIM)
        v_win = lax.dynamic_slice_in_dim(values, first, window, 0).reshape(
            window, heads_here, HEAD_DIM
        )
        seg_win = lax.dynamic_slice_in_dim(seg, first, window, 0)
        same = seg_block[:, None] == seg_win[None, :]
        mine = group_ids[:, None] == group_block[None, :]
        text_logits = jnp.einsum("qhe,khe->hqk", q_block, k_win, preferred_element_type=jnp.float32)
        text_logits = jnp.where(same[None], text_logits, jnp.float32(-1e30))
        every = jnp.einsum("qhe,gphe->hgqp", q_block, prompt_k4, preferred_element_type=jnp.float32)
        prompt_logits = jnp.sum(jnp.where(mine[None, :, :, None], every, jnp.float32(0.0)), axis=1)
        top = jnp.maximum(
            jnp.max(text_logits, axis=2, keepdims=True), jnp.max(prompt_logits, axis=2, keepdims=True)
        )
        text_w = jnp.exp(text_logits - top)
        prompt_w = jnp.exp(prompt_logits - top)
        total = jnp.sum(text_w, axis=2, keepdims=True) + jnp.sum(prompt_w, axis=2, keepdims=True)
        text_p = (text_w / total).astype(jnp.bfloat16)
        prompt_p = (prompt_w / total).astype(jnp.bfloat16)
        spread = jnp.where(mine[None, :, :, None], prompt_p[:, None], jnp.bfloat16(0))
        mixed = jnp.einsum("hqk,khe->qhe", text_p, v_win, preferred_element_type=jnp.float32)
        mixed = mixed + jnp.einsum(
            "hgqp,gphe->qhe", spread, prompt_v4, preferred_element_type=jnp.float32
        )
        return mixed.astype(jnp.bfloat16).reshape(block, columns)

    context = lax.map(attend, jnp.arange(tok_dev // block, dtype=jnp.int32)).reshape(
        tok_dev, columns
    )
    my_start = lax.axis_index("tensor") * shard_rows
    attn_part = lax.psum_scatter(
        jnp.dot(context, w_out, preferred_element_type=jnp.float32).astype(jnp.bfloat16),
        "tensor",
        scatter_dimension=0,
        tiled=True,
    ).astype(jnp.float32)
    normed_rows = layer_norm(
        tokens.astype(jnp.float32) + attn_part, norm_gain[0], norm_bias[0]
    ).astype(jnp.bfloat16)
    expanded = jax.nn.gelu(
        jnp.dot(
            lax.all_gather(normed_rows, "tensor", axis=0, tiled=True),
            w_in,
            preferred_element_type=jnp.float32,
        )
        + b_in,
        approximate=False,
    ).astype(jnp.bfloat16)
    reduced = lax.psum_scatter(
        jnp.dot(expanded, w_down, preferred_element_type=jnp.float32).astype(jnp.bfloat16),
        "tensor",
        scatter_dimension=0,
        tiled=True,
    ).astype(jnp.float32)
    output = layer_norm(
        normed_rows.astype(jnp.float32) + reduced, norm_gain[1], norm_bias[1]
    ).astype(jnp.bfloat16)
    seg_rows = lax.dynamic_slice_in_dim(seg, my_start, shard_rows, 0)
    member = (text_ids[:, None] == seg_rows[None, :]).astype(jnp.bfloat16)
    partial_sums = jnp.dot(member, output, preferred_element_type=jnp.float32)
    pooled_sums = lax.psum_scatter(partial_sums, "tensor", scatter_dimension=0, tiled=True)
    mine = pooled_sums.shape[0]
    my_lens = lax.dynamic_slice_in_dim(lens, lax.axis_index("tensor") * mine, mine, 0)
    pooled = pooled_sums / my_lens[:, None].astype(jnp.float32)
    square = jnp.mean(pooled * pooled, axis=1, keepdims=True)
    embedding = (pooled * lax.rsqrt(square + 1e-06)).astype(jnp.bfloat16)
    asked_vectors = lax.all_to_all(
        jnp.broadcast_to(embedding[None], (n_dp,) + embedding.shape), "dp", 0, 0, tiled=True
    ).reshape(-1, embedding.shape[1])
    asked_rows = lax.all_to_all(
        jnp.broadcast_to(candidates[None], (n_dp,) + candidates.shape), "dp", 0, 0, tiled=True
    ).reshape(-1, candidates.shape[1])
    held = index_rows.shape[0]
    local_rows = asked_rows - lax.axis_index("dp") * held
    table = jnp.dot(asked_vectors, index_rows.T, preferred_element_type=jnp.float32) * D ** (-0.5)
    row_ids = jnp.arange(held, dtype=jnp.int32)
    picked = jnp.sum(
        jnp.where(local_rows[:, :, None] == row_ids[None, None, :], table[:, None, :], jnp.float32(0.0)),
        axis=2,
    )
    returned = lax.all_to_all(picked, "dp", 0, 0, tiled=True)
    return jnp.sum(returned.reshape(n_dp, -1, returned.shape[1]), axis=0)


def solution(mesh):
    placed = (
        P(("dp", "tensor"), None),
        P("dp", None, None),
        P(None, None, "tensor"),
        P("tensor", None),
        P(),
        P(),
        P(None, "tensor"),
        P("tensor"),
        P("tensor", None),
        P("dp", None),
        P("dp", None),
        P("dp"),
        P(("dp", "tensor"), None),
    )
    return jax.shard_map(
        shards, mesh=mesh, in_specs=placed, out_specs=P(("dp", "tensor"), None), check_vma=False
    )
```

```python
import jax
import jax.numpy as jnp
from jax import lax
from jax.sharding import PartitionSpec as P
import functools
from jax.experimental import pallas as pl
from jax.experimental.pallas import tpu as pltpu


D = 1024
HEAD_DIM = 64


def attention_kernel(first_ref, q_ref, k_ref, v_ref, pk_ref, pv_ref, segq_ref, segw_ref, grpq_ref, kgrp_ref, o_ref, *, window):
    b = pl.program_id(1)
    f = pl.multiple_of(first_ref[b], 128)
    q = q_ref[0]
    kw = k_ref[0, pl.ds(f, window), :]
    vw = v_ref[0, pl.ds(f, window), :]
    nt = (((1,), (1,)), ((), ()))
    lt = lax.dot_general(q, kw, nt, preferred_element_type=jnp.float32)
    lt = jnp.where(segq_ref[...] == segw_ref[0], lt, jnp.float32(-1e30))
    lp = lax.dot_general(q, pk_ref[0], nt, preferred_element_type=jnp.float32)
    lp = jnp.where(grpq_ref[...] == kgrp_ref[...], lp, jnp.float32(-1e30))
    top = jnp.maximum(jnp.max(lt, axis=1, keepdims=True), jnp.max(lp, axis=1, keepdims=True))
    wt = jnp.exp(lt - top)
    wp = jnp.exp(lp - top)
    total = jnp.sum(wt, axis=1, keepdims=True) + jnp.sum(wp, axis=1, keepdims=True)
    pt = (wt / total).astype(jnp.bfloat16)
    pp = (wp / total).astype(jnp.bfloat16)
    out = jnp.dot(pt, vw, preferred_element_type=jnp.float32) + jnp.dot(
        pp, pv_ref[0], preferred_element_type=jnp.float32)
    o_ref[0] = out.astype(jnp.bfloat16)

def attention(query, keys, values, prompt_key, prompt_value, seg, tok_group, starts, prompt_len, head_dim, interpret=False):
    tok, cols = query.shape
    heads = cols // head_dim
    block = 256
    window = 1408
    nb = tok // block
    prow = prompt_key.shape[0]
    def by_head(x):
        return x.reshape(x.shape[0], heads, head_dim).transpose(1, 0, 2)
    first = jnp.clip((starts[seg[::block]] // 128) * 128, 0, tok - window).astype(jnp.int32)
    segw = jnp.take(seg, first[:, None] + jnp.arange(window, dtype=jnp.int32)[None, :], axis=0).reshape(nb, 1, window)
    segq = seg.reshape(tok, 1)
    grpq = tok_group.reshape(tok, 1)
    kgrp = (jnp.arange(prow, dtype=jnp.int32) // prompt_len).reshape(1, prow)
    grid_spec = pltpu.PrefetchScalarGridSpec(
        num_scalar_prefetch=1,
        grid=(heads, nb),
        in_specs=[
            pl.BlockSpec((1, block, head_dim), lambda h, b, fr: (h, b, 0)),
            pl.BlockSpec((1, tok, head_dim), lambda h, b, fr: (h, 0, 0)),
            pl.BlockSpec((1, tok, head_dim), lambda h, b, fr: (h, 0, 0)),
            pl.BlockSpec((1, prow, head_dim), lambda h, b, fr: (h, 0, 0)),
            pl.BlockSpec((1, prow, head_dim), lambda h, b, fr: (h, 0, 0)),
            pl.BlockSpec((block, 1), lambda h, b, fr: (b, 0)),
            pl.BlockSpec((1, 1, window), lambda h, b, fr: (b, 0, 0)),
            pl.BlockSpec((block, 1), lambda h, b, fr: (b, 0)),
            pl.BlockSpec((1, prow), lambda h, b, fr: (0, 0)),
        ],
        out_specs=pl.BlockSpec((1, block, head_dim), lambda h, b, fr: (h, b, 0)),
    )
    out = pl.pallas_call(
        functools.partial(attention_kernel, window=window),
        grid_spec=grid_spec,
        out_shape=jax.ShapeDtypeStruct((heads, tok, head_dim), jnp.bfloat16),
        interpret=interpret,
    )(first, by_head(query), by_head(keys), by_head(values), by_head(prompt_key), by_head(prompt_value), segq, segw, grpq, kgrp)
    return out.transpose(1, 0, 2).reshape(tok, cols)


def layer_norm(values, gain, bias):
    mean = jnp.mean(values, axis=-1, keepdims=True)
    centred = values - mean
    var = jnp.mean(centred * centred, axis=-1, keepdims=True)
    return centred * lax.rsqrt(var + 1e-05) * gain + bias


def project(block, weight):
    return jnp.dot(block, weight, preferred_element_type=jnp.float32).astype(jnp.bfloat16)


def shards(
    tokens,
    prompts,
    w_attn,
    w_out,
    norm_gain,
    norm_bias,
    w_in,
    b_in,
    w_down,
    index_rows,
    lengths,
    groups,
    candidates,
):
    shard_rows = tokens.shape[0]
    tok_dev = shard_rows * lax.axis_size("tensor")
    columns = w_attn.shape[2]
    heads_here = columns // HEAD_DIM
    scale = HEAD_DIM ** (-0.5)
    whole = lax.all_gather(tokens, "tensor", axis=0, tiled=True)
    query = (jnp.dot(whole, w_attn[0], preferred_element_type=jnp.float32) * scale).astype(
        jnp.bfloat16
    )
    keys = project(whole, w_attn[1])
    values = project(whole, w_attn[2])
    n_dp = lax.axis_size("dp")
    own_prompt = prompts.reshape(-1, prompts.shape[2])
    own_kv = jnp.concatenate([project(own_prompt, w_attn[1]), project(own_prompt, w_attn[2])], axis=1)
    every_kv = lax.all_to_all(
        jnp.broadcast_to(own_kv[None], (n_dp,) + own_kv.shape), "dp", 0, 0, tiled=True
    ).reshape(-1, 2 * columns)
    prompt_key = every_kv[:, :columns]
    prompt_value = every_kv[:, columns:]
    prompt_len = prompts.shape[1]
    prompt_rows = prompt_key.shape[0]
    lens = lengths[0]
    texts_here = lens.shape[0]
    text_ids = jnp.arange(texts_here, dtype=jnp.int32)
    ends = jnp.cumsum(lens)
    position = jnp.arange(tok_dev, dtype=jnp.int32)
    seg = jnp.sum((position[:, None] >= ends[None, :]).astype(jnp.int32), axis=1)
    tok_group = jnp.sum(jnp.where(seg[:, None] == text_ids[None, :], groups[None, :], 0), axis=1)
    starts = ends - lens
    context = attention(
        query, keys, values, prompt_key, prompt_value, seg, tok_group, starts, prompt_len, HEAD_DIM
    )
    my_start = lax.axis_index("tensor") * shard_rows
    attn_part = lax.psum_scatter(
        jnp.dot(context, w_out, preferred_element_type=jnp.float32).astype(jnp.bfloat16),
        "tensor",
        scatter_dimension=0,
        tiled=True,
    ).astype(jnp.float32)
    normed_rows = layer_norm(
        tokens.astype(jnp.float32) + attn_part, norm_gain[0], norm_bias[0]
    ).astype(jnp.bfloat16)
    expanded = jax.nn.gelu(
        jnp.dot(
            lax.all_gather(normed_rows, "tensor", axis=0, tiled=True),
            w_in,
            preferred_element_type=jnp.float32,
        )
        + b_in,
        approximate=False,
    ).astype(jnp.bfloat16)
    reduced = lax.psum_scatter(
        jnp.dot(expanded, w_down, preferred_element_type=jnp.float32).astype(jnp.bfloat16),
        "tensor",
        scatter_dimension=0,
        tiled=True,
    ).astype(jnp.float32)
    output = layer_norm(
        normed_rows.astype(jnp.float32) + reduced, norm_gain[1], norm_bias[1]
    ).astype(jnp.bfloat16)
    seg_rows = lax.dynamic_slice_in_dim(seg, my_start, shard_rows, 0)
    member = (text_ids[:, None] == seg_rows[None, :]).astype(jnp.bfloat16)
    partial_sums = jnp.dot(member, output, preferred_element_type=jnp.float32)
    pooled_sums = lax.psum_scatter(partial_sums, "tensor", scatter_dimension=0, tiled=True)
    mine = pooled_sums.shape[0]
    my_lens = lax.dynamic_slice_in_dim(lens, lax.axis_index("tensor") * mine, mine, 0)
    pooled = pooled_sums / my_lens[:, None].astype(jnp.float32)
    square = jnp.mean(pooled * pooled, axis=1, keepdims=True)
    embedding = (pooled * lax.rsqrt(square + 1e-06)).astype(jnp.bfloat16)
    asked_vectors = lax.all_to_all(
        jnp.broadcast_to(embedding[None], (n_dp,) + embedding.shape), "dp", 0, 0, tiled=True
    ).reshape(-1, embedding.shape[1])
    asked_rows = lax.all_to_all(
        jnp.broadcast_to(candidates[None], (n_dp,) + candidates.shape), "dp", 0, 0, tiled=True
    ).reshape(-1, candidates.shape[1])
    held = index_rows.shape[0]
    local_rows = asked_rows - lax.axis_index("dp") * held
    table = jnp.dot(asked_vectors, index_rows.T, preferred_element_type=jnp.float32) * D ** (-0.5)
    row_ids = jnp.arange(held, dtype=jnp.int32)
    picked = jnp.sum(
        jnp.where(local_rows[:, :, None] == row_ids[None, None, :], table[:, None, :], jnp.float32(0.0)),
        axis=2,
    )
    returned = lax.all_to_all(picked, "dp", 0, 0, tiled=True)
    return jnp.sum(returned.reshape(n_dp, -1, returned.shape[1]), axis=0)


def solution(mesh):
    placed = (
        P(("dp", "tensor"), None),
        P("dp", None, None),
        P(None, None, "tensor"),
        P("tensor", None),
        P(),
        P(),
        P(None, "tensor"),
        P("tensor"),
        P("tensor", None),
        P("dp", None),
        P("dp", None),
        P("dp"),
        P(("dp", "tensor"), None),
    )
    return jax.shard_map(
        shards, mesh=mesh, in_specs=placed, out_specs=P(("dp", "tensor"), None), check_vma=False
    )
```

```python
import jax
import jax.numpy as jnp
from jax import lax
from jax.sharding import PartitionSpec as P
import functools
from jax.experimental import pallas as pl
from jax.experimental.pallas import tpu as pltpu


D = 1024
HEAD_DIM = 64


def attention_kernel(first_ref, q_ref, k_ref, v_ref, pk_ref, pv_ref, segq_ref, segw_ref, grpq_ref, kgrp_ref, o_ref, *, window):
    b = pl.program_id(1)
    f = pl.multiple_of(first_ref[b], 128)
    q = q_ref[0]
    kw = k_ref[0, pl.ds(f, window), :]
    vw = v_ref[0, pl.ds(f, window), :]
    nt = (((1,), (1,)), ((), ()))
    lt = lax.dot_general(q, kw, nt, preferred_element_type=jnp.float32)
    lt = jnp.where(segq_ref[...] == segw_ref[0], lt, jnp.float32(-1e30))
    lp = lax.dot_general(q, pk_ref[0], nt, preferred_element_type=jnp.float32)
    lp = jnp.where(grpq_ref[...] == kgrp_ref[...], lp, jnp.float32(-1e30))
    top = jnp.maximum(jnp.max(lt, axis=1, keepdims=True), jnp.max(lp, axis=1, keepdims=True))
    wt = jnp.exp(lt - top)
    wp = jnp.exp(lp - top)
    total = jnp.sum(wt, axis=1, keepdims=True) + jnp.sum(wp, axis=1, keepdims=True)
    pt = (wt / total).astype(jnp.bfloat16)
    pp = (wp / total).astype(jnp.bfloat16)
    out = jnp.dot(pt, vw, preferred_element_type=jnp.float32) + jnp.dot(
        pp, pv_ref[0], preferred_element_type=jnp.float32)
    o_ref[0] = out.astype(jnp.bfloat16)

def attention(query, keys, values, prompt_key, prompt_value, seg, tok_group, ends, starts, prompt_len, head_dim, interpret=False):
    tok, cols = query.shape
    heads = cols // head_dim
    block = 256
    window = 1408
    nb = tok // block
    prow = prompt_key.shape[0]
    def by_head(x):
        return x.reshape(x.shape[0], heads, head_dim).transpose(1, 0, 2)
    first = jnp.clip((starts[seg[::block]] // 128) * 128, 0, tok - window).astype(jnp.int32)
    at = first[:, None] + jnp.arange(window, dtype=jnp.int32)[None, :]
    segw = jnp.sum((at[:, :, None] >= ends[None, None, :]).astype(jnp.int32), axis=2).reshape(nb, 1, window)
    segq = seg.reshape(tok, 1)
    grpq = tok_group.reshape(tok, 1)
    kgrp = (jnp.arange(prow, dtype=jnp.int32) // prompt_len).reshape(1, prow)
    grid_spec = pltpu.PrefetchScalarGridSpec(
        num_scalar_prefetch=1,
        grid=(heads, nb),
        in_specs=[
            pl.BlockSpec((1, block, head_dim), lambda h, b, fr: (h, b, 0)),
            pl.BlockSpec((1, tok, head_dim), lambda h, b, fr: (h, 0, 0)),
            pl.BlockSpec((1, tok, head_dim), lambda h, b, fr: (h, 0, 0)),
            pl.BlockSpec((1, prow, head_dim), lambda h, b, fr: (h, 0, 0)),
            pl.BlockSpec((1, prow, head_dim), lambda h, b, fr: (h, 0, 0)),
            pl.BlockSpec((block, 1), lambda h, b, fr: (b, 0)),
            pl.BlockSpec((1, 1, window), lambda h, b, fr: (b, 0, 0)),
            pl.BlockSpec((block, 1), lambda h, b, fr: (b, 0)),
            pl.BlockSpec((1, prow), lambda h, b, fr: (0, 0)),
        ],
        out_specs=pl.BlockSpec((1, block, head_dim), lambda h, b, fr: (h, b, 0)),
    )
    out = pl.pallas_call(
        functools.partial(attention_kernel, window=window),
        grid_spec=grid_spec,
        out_shape=jax.ShapeDtypeStruct((heads, tok, head_dim), jnp.bfloat16),
        interpret=interpret,
    )(first, by_head(query), by_head(keys), by_head(values), by_head(prompt_key), by_head(prompt_value), segq, segw, grpq, kgrp)
    return out.transpose(1, 0, 2).reshape(tok, cols)


def layer_norm(values, gain, bias):
    mean = jnp.mean(values, axis=-1, keepdims=True)
    centred = values - mean
    var = jnp.mean(centred * centred, axis=-1, keepdims=True)
    return centred * lax.rsqrt(var + 1e-05) * gain + bias


def project(block, weight):
    return jnp.dot(block, weight, preferred_element_type=jnp.float32).astype(jnp.bfloat16)


def shards(
    tokens,
    prompts,
    w_attn,
    w_out,
    norm_gain,
    norm_bias,
    w_in,
    b_in,
    w_down,
    index_rows,
    lengths,
    groups,
    candidates,
):
    shard_rows = tokens.shape[0]
    tok_dev = shard_rows * lax.axis_size("tensor")
    columns = w_attn.shape[2]
    heads_here = columns // HEAD_DIM
    scale = HEAD_DIM ** (-0.5)
    whole = lax.all_gather(tokens, "tensor", axis=0, tiled=True)
    query = (jnp.dot(whole, w_attn[0], preferred_element_type=jnp.float32) * scale).astype(
        jnp.bfloat16
    )
    keys = project(whole, w_attn[1])
    values = project(whole, w_attn[2])
    n_dp = lax.axis_size("dp")
    own_prompt = prompts.reshape(-1, prompts.shape[2])
    own_kv = jnp.concatenate([project(own_prompt, w_attn[1]), project(own_prompt, w_attn[2])], axis=1)
    every_kv = lax.all_to_all(
        jnp.broadcast_to(own_kv[None], (n_dp,) + own_kv.shape), "dp", 0, 0, tiled=True
    ).reshape(-1, 2 * columns)
    prompt_key = every_kv[:, :columns]
    prompt_value = every_kv[:, columns:]
    prompt_len = prompts.shape[1]
    prompt_rows = prompt_key.shape[0]
    lens = lengths[0]
    texts_here = lens.shape[0]
    text_ids = jnp.arange(texts_here, dtype=jnp.int32)
    ends = jnp.cumsum(lens)
    position = jnp.arange(tok_dev, dtype=jnp.int32)
    seg = jnp.sum((position[:, None] >= ends[None, :]).astype(jnp.int32), axis=1)
    tok_group = jnp.sum(jnp.where(seg[:, None] == text_ids[None, :], groups[None, :], 0), axis=1)
    starts = ends - lens
    context = attention(
        query, keys, values, prompt_key, prompt_value, seg, tok_group, ends, starts, prompt_len, HEAD_DIM
    )
    my_start = lax.axis_index("tensor") * shard_rows
    attn_part = lax.psum_scatter(
        jnp.dot(context, w_out, preferred_element_type=jnp.float32).astype(jnp.bfloat16),
        "tensor",
        scatter_dimension=0,
        tiled=True,
    ).astype(jnp.float32)
    asked_rows = lax.all_to_all(
        jnp.broadcast_to(candidates[None], (n_dp,) + candidates.shape), "dp", 0, 0, tiled=True
    ).reshape(-1, candidates.shape[1])
    asked_rows, attn_part = lax.optimization_barrier((asked_rows, attn_part))
    normed_rows = layer_norm(
        tokens.astype(jnp.float32) + attn_part, norm_gain[0], norm_bias[0]
    ).astype(jnp.bfloat16)
    expanded = jax.nn.gelu(
        jnp.dot(
            lax.all_gather(normed_rows, "tensor", axis=0, tiled=True),
            w_in,
            preferred_element_type=jnp.float32,
        )
        + b_in,
        approximate=False,
    ).astype(jnp.bfloat16)
    reduced = lax.psum_scatter(
        jnp.dot(expanded, w_down, preferred_element_type=jnp.float32).astype(jnp.bfloat16),
        "tensor",
        scatter_dimension=0,
        tiled=True,
    ).astype(jnp.float32)
    output = layer_norm(
        normed_rows.astype(jnp.float32) + reduced, norm_gain[1], norm_bias[1]
    ).astype(jnp.bfloat16)
    seg_rows = lax.dynamic_slice_in_dim(seg, my_start, shard_rows, 0)
    member = (text_ids[:, None] == seg_rows[None, :]).astype(jnp.bfloat16)
    partial_sums = jnp.dot(member, output, preferred_element_type=jnp.float32)
    pooled_sums = lax.psum_scatter(partial_sums, "tensor", scatter_dimension=0, tiled=True)
    mine = pooled_sums.shape[0]
    my_lens = lax.dynamic_slice_in_dim(lens, lax.axis_index("tensor") * mine, mine, 0)
    pooled = pooled_sums / my_lens[:, None].astype(jnp.float32)
    square = jnp.mean(pooled * pooled, axis=1, keepdims=True)
    embedding = (pooled * lax.rsqrt(square + 1e-06)).astype(jnp.bfloat16)
    asked_vectors = lax.all_to_all(
        jnp.broadcast_to(embedding[None], (n_dp,) + embedding.shape), "dp", 0, 0, tiled=True
    ).reshape(-1, embedding.shape[1])
    held = index_rows.shape[0]
    local_rows = asked_rows - lax.axis_index("dp") * held
    table = jnp.dot(asked_vectors, index_rows.T, preferred_element_type=jnp.float32) * D ** (-0.5)
    row_ids = jnp.arange(held, dtype=jnp.int32)
    picked = jnp.sum(
        jnp.where(local_rows[:, :, None] == row_ids[None, None, :], table[:, None, :], jnp.float32(0.0)),
        axis=2,
    )
    returned = lax.all_to_all(picked, "dp", 0, 0, tiled=True)
    return jnp.sum(returned.reshape(n_dp, -1, returned.shape[1]), axis=0)


def solution(mesh):
    placed = (
        P(("dp", "tensor"), None),
        P("dp", None, None),
        P(None, None, "tensor"),
        P("tensor", None),
        P(),
        P(),
        P(None, "tensor"),
        P("tensor"),
        P("tensor", None),
        P("dp", None),
        P("dp", None),
        P("dp"),
        P(("dp", "tensor"), None),
    )
    return jax.shard_map(
        shards, mesh=mesh, in_specs=placed, out_specs=P(("dp", "tensor"), None), check_vma=False
    )
```

```python
import jax
import jax.numpy as jnp
from jax import lax
from jax.sharding import PartitionSpec as P
import functools
from jax.experimental import pallas as pl
from jax.experimental.pallas import tpu as pltpu


D = 1024
HEAD_DIM = 64


def attention_kernel(first_ref, q_ref, k_ref, v_ref, pk_ref, pv_ref, segq_ref, segw_ref, grpq_ref, kgrp_ref, o_ref, *, window):
    b = pl.program_id(1)
    f = pl.multiple_of(first_ref[b], 128)
    q = q_ref[0]
    kw = k_ref[0, pl.ds(f, window), :]
    vw = v_ref[0, pl.ds(f, window), :]
    nt = (((1,), (1,)), ((), ()))
    lt = lax.dot_general(q, kw, nt, preferred_element_type=jnp.float32)
    lt = jnp.where(segq_ref[...] == segw_ref[0], lt, jnp.float32(-1e30))
    lp = lax.dot_general(q, pk_ref[0], nt, preferred_element_type=jnp.float32)
    lp = jnp.where(grpq_ref[...] == kgrp_ref[...], lp, jnp.float32(-1e30))
    top = jnp.maximum(jnp.max(lt, axis=1, keepdims=True), jnp.max(lp, axis=1, keepdims=True))
    wt = jnp.exp(lt - top)
    wp = jnp.exp(lp - top)
    total = jnp.sum(wt, axis=1, keepdims=True) + jnp.sum(wp, axis=1, keepdims=True)
    pt = (wt / total).astype(jnp.bfloat16)
    pp = (wp / total).astype(jnp.bfloat16)
    out = jnp.dot(pt, vw, preferred_element_type=jnp.float32) + jnp.dot(
        pp, pv_ref[0], preferred_element_type=jnp.float32)
    o_ref[0] = out.astype(jnp.bfloat16)

def attention(query, keys, values, prompt_key, prompt_value, seg, tok_group, ends, starts, prompt_len, head_dim, parity=0, halves=1, interpret=False):
    tok, cols = query.shape
    heads = cols // head_dim
    block = 256
    window = 1408
    nb = tok // block
    prow = prompt_key.shape[0]
    def by_head(x):
        return x.reshape(x.shape[0], heads, head_dim).transpose(1, 0, 2)
    first = jnp.clip((starts[seg[::block]] // 128) * 128, 0, tok - window).astype(jnp.int32)
    at = first[:, None] + jnp.arange(window, dtype=jnp.int32)[None, :]
    segw = jnp.sum((at[:, :, None] >= ends[None, None, :]).astype(jnp.int32), axis=2).reshape(nb, 1, window)
    segq = seg.reshape(tok, 1)
    grpq = tok_group.reshape(tok, 1)
    kgrp = (jnp.arange(prow, dtype=jnp.int32) // prompt_len).reshape(1, prow)
    first = first[parity::halves]
    segw = segw[parity::halves]
    grid_spec = pltpu.PrefetchScalarGridSpec(
        num_scalar_prefetch=1,
        grid=(heads, nb // halves),
        in_specs=[
            pl.BlockSpec((1, block, head_dim), lambda h, b, fr: (h, halves * b + parity, 0)),
            pl.BlockSpec((1, tok, head_dim), lambda h, b, fr: (h, 0, 0)),
            pl.BlockSpec((1, tok, head_dim), lambda h, b, fr: (h, 0, 0)),
            pl.BlockSpec((1, prow, head_dim), lambda h, b, fr: (h, 0, 0)),
            pl.BlockSpec((1, prow, head_dim), lambda h, b, fr: (h, 0, 0)),
            pl.BlockSpec((block, 1), lambda h, b, fr: (halves * b + parity, 0)),
            pl.BlockSpec((1, 1, window), lambda h, b, fr: (b, 0, 0)),
            pl.BlockSpec((block, 1), lambda h, b, fr: (halves * b + parity, 0)),
            pl.BlockSpec((1, prow), lambda h, b, fr: (0, 0)),
        ],
        out_specs=pl.BlockSpec((1, block, head_dim), lambda h, b, fr: (h, b, 0)),
    )
    out = pl.pallas_call(
        functools.partial(attention_kernel, window=window),
        grid_spec=grid_spec,
        out_shape=jax.ShapeDtypeStruct((heads, tok // halves, head_dim), jnp.bfloat16),
        interpret=interpret,
    )(first, by_head(query), by_head(keys), by_head(values), by_head(prompt_key), by_head(prompt_value), segq, segw, grpq, kgrp)
    return out.transpose(1, 0, 2).reshape(tok // halves, cols)


def layer_norm(values, gain, bias):
    mean = jnp.mean(values, axis=-1, keepdims=True)
    centred = values - mean
    var = jnp.mean(centred * centred, axis=-1, keepdims=True)
    return centred * lax.rsqrt(var + 1e-05) * gain + bias


def project(block, weight):
    return jnp.dot(block, weight, preferred_element_type=jnp.float32).astype(jnp.bfloat16)


def shards(
    tokens,
    prompts,
    w_attn,
    w_out,
    norm_gain,
    norm_bias,
    w_in,
    b_in,
    w_down,
    index_rows,
    lengths,
    groups,
    candidates,
):
    shard_rows = tokens.shape[0]
    tok_dev = shard_rows * lax.axis_size("tensor")
    columns = w_attn.shape[2]
    heads_here = columns // HEAD_DIM
    scale = HEAD_DIM ** (-0.5)
    whole = lax.all_gather(tokens, "tensor", axis=0, tiled=True)
    query = (jnp.dot(whole, w_attn[0], preferred_element_type=jnp.float32) * scale).astype(
        jnp.bfloat16
    )
    keys = project(whole, w_attn[1])
    values = project(whole, w_attn[2])
    n_dp = lax.axis_size("dp")
    own_prompt = prompts.reshape(-1, prompts.shape[2])
    own_kv = jnp.concatenate([project(own_prompt, w_attn[1]), project(own_prompt, w_attn[2])], axis=1)
    every_kv = lax.all_to_all(
        jnp.broadcast_to(own_kv[None], (n_dp,) + own_kv.shape), "dp", 0, 0, tiled=True
    ).reshape(-1, 2 * columns)
    prompt_key = every_kv[:, :columns]
    prompt_value = every_kv[:, columns:]
    prompt_len = prompts.shape[1]
    prompt_rows = prompt_key.shape[0]
    lens = lengths[0]
    texts_here = lens.shape[0]
    text_ids = jnp.arange(texts_here, dtype=jnp.int32)
    ends = jnp.cumsum(lens)
    position = jnp.arange(tok_dev, dtype=jnp.int32)
    seg = jnp.sum((position[:, None] >= ends[None, :]).astype(jnp.int32), axis=1)
    tok_group = jnp.sum(jnp.where(seg[:, None] == text_ids[None, :], groups[None, :], 0), axis=1)
    starts = ends - lens
    my_start = lax.axis_index("tensor") * shard_rows

    def attend_half(parity):
        context = attention(
            query, keys, values, prompt_key, prompt_value, seg, tok_group, ends, starts, prompt_len,
            HEAD_DIM, parity=parity, halves=2,
        )
        return lax.psum_scatter(
            jnp.dot(context, w_out, preferred_element_type=jnp.float32).astype(jnp.bfloat16),
            "tensor",
            scatter_dimension=0,
            tiled=True,
        ).astype(jnp.float32)

    attn_part = jnp.concatenate([attend_half(0), attend_half(1)], axis=0)
    asked_rows = lax.all_to_all(
        jnp.broadcast_to(candidates[None], (n_dp,) + candidates.shape), "dp", 0, 0, tiled=True
    ).reshape(-1, candidates.shape[1])
    asked_rows, attn_part = lax.optimization_barrier((asked_rows, attn_part))
    normed_rows = layer_norm(
        tokens.astype(jnp.float32) + attn_part, norm_gain[0], norm_bias[0]
    ).astype(jnp.bfloat16)
    half_rows = shard_rows // 2

    def feed_half(rows):
        expanded = jax.nn.gelu(
            jnp.dot(
                lax.all_gather(rows, "tensor", axis=0, tiled=True),
                w_in,
                preferred_element_type=jnp.float32,
            )
            + b_in,
            approximate=False,
        ).astype(jnp.bfloat16)
        return lax.psum_scatter(
            jnp.dot(expanded, w_down, preferred_element_type=jnp.float32).astype(jnp.bfloat16),
            "tensor",
            scatter_dimension=0,
            tiled=True,
        ).astype(jnp.float32)

    reduced = jnp.concatenate(
        [feed_half(normed_rows[:half_rows]), feed_half(normed_rows[half_rows:])], axis=0
    )
    output = layer_norm(
        normed_rows.astype(jnp.float32) + reduced, norm_gain[1], norm_bias[1]
    ).astype(jnp.bfloat16)
    seg_rows = lax.dynamic_slice_in_dim(seg, my_start, shard_rows, 0)
    member = (text_ids[:, None] == seg_rows[None, :]).astype(jnp.bfloat16)
    partial_sums = jnp.dot(member, output, preferred_element_type=jnp.float32)
    pooled_sums = lax.psum_scatter(partial_sums, "tensor", scatter_dimension=0, tiled=True)
    mine = pooled_sums.shape[0]
    my_lens = lax.dynamic_slice_in_dim(lens, lax.axis_index("tensor") * mine, mine, 0)
    pooled = pooled_sums / my_lens[:, None].astype(jnp.float32)
    square = jnp.mean(pooled * pooled, axis=1, keepdims=True)
    embedding = (pooled * lax.rsqrt(square + 1e-06)).astype(jnp.bfloat16)
    asked_vectors = lax.all_to_all(
        jnp.broadcast_to(embedding[None], (n_dp,) + embedding.shape), "dp", 0, 0, tiled=True
    ).reshape(-1, embedding.shape[1])
    held = index_rows.shape[0]
    local_rows = asked_rows - lax.axis_index("dp") * held
    table = jnp.dot(asked_vectors, index_rows.T, preferred_element_type=jnp.float32) * D ** (-0.5)
    row_ids = jnp.arange(held, dtype=jnp.int32)
    picked = jnp.sum(
        jnp.where(local_rows[:, :, None] == row_ids[None, None, :], table[:, None, :], jnp.float32(0.0)),
        axis=2,
    )
    returned = lax.all_to_all(picked, "dp", 0, 0, tiled=True)
    return jnp.sum(returned.reshape(n_dp, -1, returned.shape[1]), axis=0)


def solution(mesh):
    placed = (
        P(("dp", "tensor"), None),
        P("dp", None, None),
        P(None, None, "tensor"),
        P("tensor", None),
        P(),
        P(),
        P(None, "tensor"),
        P("tensor"),
        P("tensor", None),
        P("dp", None),
        P("dp", None),
        P("dp"),
        P(("dp", "tensor"), None),
    )
    return jax.shard_map(
        shards, mesh=mesh, in_specs=placed, out_specs=P(("dp", "tensor"), None), check_vma=False
    )
```

```python
import jax
import jax.numpy as jnp
from jax import lax
from jax.sharding import PartitionSpec as P
import functools
from jax.experimental import pallas as pl
from jax.experimental.pallas import tpu as pltpu


D = 1024
HEAD_DIM = 64


def attention_kernel(first_ref, q_ref, k_ref, v_ref, pk_ref, pv_ref, segq_ref, segw_ref, grpq_ref, kgrp_ref, o_ref, *, window):
    b = pl.program_id(1)
    f = pl.multiple_of(first_ref[b], 128)
    q = q_ref[0]
    kw = k_ref[0, pl.ds(f, window), :]
    vw = v_ref[0, pl.ds(f, window), :]
    nt = (((1,), (1,)), ((), ()))
    lt = lax.dot_general(q, kw, nt, preferred_element_type=jnp.float32)
    lt = jnp.where(segq_ref[...] == segw_ref[0], lt, jnp.float32(-1e30))
    lp = lax.dot_general(q, pk_ref[0], nt, preferred_element_type=jnp.float32)
    lp = jnp.where(grpq_ref[...] == kgrp_ref[...], lp, jnp.float32(-1e30))
    top = jnp.maximum(jnp.max(lt, axis=1, keepdims=True), jnp.max(lp, axis=1, keepdims=True))
    wt = jnp.exp(lt - top)
    wp = jnp.exp(lp - top)
    total = jnp.sum(wt, axis=1, keepdims=True) + jnp.sum(wp, axis=1, keepdims=True)
    pt = (wt / total).astype(jnp.bfloat16)
    pp = (wp / total).astype(jnp.bfloat16)
    out = jnp.dot(pt, vw, preferred_element_type=jnp.float32) + jnp.dot(
        pp, pv_ref[0], preferred_element_type=jnp.float32)
    o_ref[0] = out.astype(jnp.bfloat16)

def attention(query, keys, values, prompt_key, prompt_value, seg, tok_group, ends, starts, prompt_len, head_dim, parity=0, halves=1, interpret=False):
    tok, cols = query.shape
    heads = cols // head_dim
    block = 256
    window = 1408
    nb = tok // block
    prow = prompt_key.shape[0]
    def by_head(x):
        return x.reshape(x.shape[0], heads, head_dim).transpose(1, 0, 2)
    first = jnp.clip((starts[seg[::block]] // 128) * 128, 0, tok - window).astype(jnp.int32)
    at = first[:, None] + jnp.arange(window, dtype=jnp.int32)[None, :]
    segw = jnp.sum((at[:, :, None] >= ends[None, None, :]).astype(jnp.int32), axis=2).reshape(nb, 1, window)
    segq = seg.reshape(tok, 1)
    grpq = tok_group.reshape(tok, 1)
    kgrp = (jnp.arange(prow, dtype=jnp.int32) // prompt_len).reshape(1, prow)
    first = first[parity::halves]
    segw = segw[parity::halves]
    grid_spec = pltpu.PrefetchScalarGridSpec(
        num_scalar_prefetch=1,
        grid=(heads, nb // halves),
        in_specs=[
            pl.BlockSpec((1, block, head_dim), lambda h, b, fr: (h, halves * b + parity, 0)),
            pl.BlockSpec((1, tok, head_dim), lambda h, b, fr: (h, 0, 0)),
            pl.BlockSpec((1, tok, head_dim), lambda h, b, fr: (h, 0, 0)),
            pl.BlockSpec((1, prow, head_dim), lambda h, b, fr: (h, 0, 0)),
            pl.BlockSpec((1, prow, head_dim), lambda h, b, fr: (h, 0, 0)),
            pl.BlockSpec((block, 1), lambda h, b, fr: (halves * b + parity, 0)),
            pl.BlockSpec((1, 1, window), lambda h, b, fr: (b, 0, 0)),
            pl.BlockSpec((block, 1), lambda h, b, fr: (halves * b + parity, 0)),
            pl.BlockSpec((1, prow), lambda h, b, fr: (0, 0)),
        ],
        out_specs=pl.BlockSpec((1, block, head_dim), lambda h, b, fr: (h, b, 0)),
    )
    out = pl.pallas_call(
        functools.partial(attention_kernel, window=window),
        grid_spec=grid_spec,
        out_shape=jax.ShapeDtypeStruct((heads, tok // halves, head_dim), jnp.bfloat16),
        interpret=interpret,
    )(first, by_head(query), by_head(keys), by_head(values), by_head(prompt_key), by_head(prompt_value), segq, segw, grpq, kgrp)
    return out.transpose(1, 0, 2).reshape(tok // halves, cols)

CROSS = [(0, 2), (2, 0), (1, 3), (3, 1)]
ONCHIP = [(0, 1), (1, 0), (2, 3), (3, 2)]


def gather_tensor(x):
    t = lax.axis_index("tensor")
    upper = t // 2
    core = t % 2
    y = lax.ppermute(x, "tensor", CROSS)
    low = jnp.where(upper == 0, x, y)
    high = jnp.where(upper == 0, y, x)
    pair = jnp.stack([low, high])
    other = lax.ppermute(pair, "tensor", ONCHIP)
    first = core == 0
    return jnp.concatenate(
        [
            jnp.where(first, pair[0], other[0]),
            jnp.where(first, other[0], pair[0]),
            jnp.where(first, pair[1], other[1]),
            jnp.where(first, other[1], pair[1]),
        ],
        axis=0,
    )


def scatter_tensor(part, link_dtype):
    t = lax.axis_index("tensor")
    upper = t // 2
    core = t % 2
    n = part.shape[0] // 4
    blocks = part.reshape((2, 2, n) + part.shape[1:])
    mine = lax.dynamic_index_in_dim(blocks, core, axis=1, keepdims=False)
    theirs = lax.dynamic_index_in_dim(blocks, 1 - core, axis=1, keepdims=False)
    got = lax.ppermute(theirs.astype(link_dtype), "tensor", ONCHIP)
    chip_sum = mine.astype(jnp.float32) + got.astype(jnp.float32)
    keep = lax.dynamic_index_in_dim(chip_sum, upper, axis=0, keepdims=False)
    send = lax.dynamic_index_in_dim(chip_sum, 1 - upper, axis=0, keepdims=False)
    return keep + lax.ppermute(send.astype(link_dtype), "tensor", CROSS).astype(jnp.float32)


def layer_norm(values, gain, bias):
    mean = jnp.mean(values, axis=-1, keepdims=True)
    centred = values - mean
    var = jnp.mean(centred * centred, axis=-1, keepdims=True)
    return centred * lax.rsqrt(var + 1e-05) * gain + bias


def project(block, weight):
    return jnp.dot(block, weight, preferred_element_type=jnp.float32).astype(jnp.bfloat16)


def shards(
    tokens,
    prompts,
    w_attn,
    w_out,
    norm_gain,
    norm_bias,
    w_in,
    b_in,
    w_down,
    index_rows,
    lengths,
    groups,
    candidates,
):
    shard_rows = tokens.shape[0]
    tok_dev = shard_rows * lax.axis_size("tensor")
    columns = w_attn.shape[2]
    heads_here = columns // HEAD_DIM
    scale = HEAD_DIM ** (-0.5)
    whole = gather_tensor(tokens)
    query = (jnp.dot(whole, w_attn[0], preferred_element_type=jnp.float32) * scale).astype(
        jnp.bfloat16
    )
    keys = project(whole, w_attn[1])
    values = project(whole, w_attn[2])
    n_dp = lax.axis_size("dp")
    own_prompt = prompts.reshape(-1, prompts.shape[2])
    own_kv = jnp.concatenate([project(own_prompt, w_attn[1]), project(own_prompt, w_attn[2])], axis=1)
    every_kv = lax.all_to_all(
        jnp.broadcast_to(own_kv[None], (n_dp,) + own_kv.shape), "dp", 0, 0, tiled=True
    ).reshape(-1, 2 * columns)
    prompt_key = every_kv[:, :columns]
    prompt_value = every_kv[:, columns:]
    prompt_len = prompts.shape[1]
    prompt_rows = prompt_key.shape[0]
    lens = lengths[0]
    texts_here = lens.shape[0]
    text_ids = jnp.arange(texts_here, dtype=jnp.int32)
    ends = jnp.cumsum(lens)
    position = jnp.arange(tok_dev, dtype=jnp.int32)
    seg = jnp.sum((position[:, None] >= ends[None, :]).astype(jnp.int32), axis=1)
    tok_group = jnp.sum(jnp.where(seg[:, None] == text_ids[None, :], groups[None, :], 0), axis=1)
    starts = ends - lens
    my_start = lax.axis_index("tensor") * shard_rows

    def attend_half(parity):
        context = attention(
            query, keys, values, prompt_key, prompt_value, seg, tok_group, ends, starts, prompt_len,
            HEAD_DIM, parity=parity, halves=2,
        )
        return scatter_tensor(jnp.dot(context, w_out, preferred_element_type=jnp.float32), jnp.bfloat16)

    attn_part = jnp.concatenate([attend_half(0), attend_half(1)], axis=0)
    asked_rows = lax.all_to_all(
        jnp.broadcast_to(candidates[None], (n_dp,) + candidates.shape), "dp", 0, 0, tiled=True
    ).reshape(-1, candidates.shape[1])
    asked_rows, attn_part = lax.optimization_barrier((asked_rows, attn_part))
    normed_rows = layer_norm(
        tokens.astype(jnp.float32) + attn_part, norm_gain[0], norm_bias[0]
    ).astype(jnp.bfloat16)
    half_rows = shard_rows // 2

    def feed_half(rows):
        expanded = jax.nn.gelu(
            jnp.dot(
                gather_tensor(rows),
                w_in,
                preferred_element_type=jnp.float32,
            )
            + b_in,
            approximate=False,
        ).astype(jnp.bfloat16)
        return scatter_tensor(jnp.dot(expanded, w_down, preferred_element_type=jnp.float32), jnp.bfloat16)

    reduced = jnp.concatenate(
        [feed_half(normed_rows[:half_rows]), feed_half(normed_rows[half_rows:])], axis=0
    )
    output = layer_norm(
        normed_rows.astype(jnp.float32) + reduced, norm_gain[1], norm_bias[1]
    ).astype(jnp.bfloat16)
    seg_rows = lax.dynamic_slice_in_dim(seg, my_start, shard_rows, 0)
    member = (text_ids[:, None] == seg_rows[None, :]).astype(jnp.bfloat16)
    partial_sums = jnp.dot(member, output, preferred_element_type=jnp.float32)
    pooled_sums = lax.psum_scatter(partial_sums, "tensor", scatter_dimension=0, tiled=True)
    mine = pooled_sums.shape[0]
    my_lens = lax.dynamic_slice_in_dim(lens, lax.axis_index("tensor") * mine, mine, 0)
    pooled = pooled_sums / my_lens[:, None].astype(jnp.float32)
    square = jnp.mean(pooled * pooled, axis=1, keepdims=True)
    embedding = (pooled * lax.rsqrt(square + 1e-06)).astype(jnp.bfloat16)
    asked_vectors = lax.all_to_all(
        jnp.broadcast_to(embedding[None], (n_dp,) + embedding.shape), "dp", 0, 0, tiled=True
    ).reshape(-1, embedding.shape[1])
    held = index_rows.shape[0]
    local_rows = asked_rows - lax.axis_index("dp") * held
    table = jnp.dot(asked_vectors, index_rows.T, preferred_element_type=jnp.float32) * D ** (-0.5)
    row_ids = jnp.arange(held, dtype=jnp.int32)
    picked = jnp.sum(
        jnp.where(local_rows[:, :, None] == row_ids[None, None, :], table[:, None, :], jnp.float32(0.0)),
        axis=2,
    )
    returned = lax.all_to_all(picked, "dp", 0, 0, tiled=True)
    return jnp.sum(returned.reshape(n_dp, -1, returned.shape[1]), axis=0)


def solution(mesh):
    placed = (
        P(("dp", "tensor"), None),
        P("dp", None, None),
        P(None, None, "tensor"),
        P("tensor", None),
        P(),
        P(),
        P(None, "tensor"),
        P("tensor"),
        P("tensor", None),
        P("dp", None),
        P("dp", None),
        P("dp"),
        P(("dp", "tensor"), None),
    )
    return jax.shard_map(
        shards, mesh=mesh, in_specs=placed, out_specs=P(("dp", "tensor"), None), check_vma=False
    )
```

```python
import jax
import jax.numpy as jnp
from jax import lax
from jax.sharding import PartitionSpec as P
import functools
from jax.experimental import pallas as pl
from jax.experimental.pallas import tpu as pltpu


D = 1024
HEAD_DIM = 64


def attention_kernel(first_ref, q_ref, k_ref, v_ref, pk_ref, pv_ref, segq_ref, segw_ref, grpq_ref, kgrp_ref, o_ref, *, window):
    b = pl.program_id(1)
    f = pl.multiple_of(first_ref[b], 128)
    q = q_ref[0]
    kw = k_ref[0, pl.ds(f, window), :]
    vw = v_ref[0, pl.ds(f, window), :]
    nt = (((1,), (1,)), ((), ()))
    lt = lax.dot_general(q, kw, nt, preferred_element_type=jnp.float32)
    lt = jnp.where(segq_ref[...] == segw_ref[0], lt, jnp.float32(-1e30))
    lp = lax.dot_general(q, pk_ref[0], nt, preferred_element_type=jnp.float32)
    lp = jnp.where(grpq_ref[...] == kgrp_ref[...], lp, jnp.float32(-1e30))
    top = jnp.maximum(jnp.max(lt, axis=1, keepdims=True), jnp.max(lp, axis=1, keepdims=True))
    wt = jnp.exp(lt - top)
    wp = jnp.exp(lp - top)
    total = jnp.sum(wt, axis=1, keepdims=True) + jnp.sum(wp, axis=1, keepdims=True)
    pt = (wt / total).astype(jnp.bfloat16)
    pp = (wp / total).astype(jnp.bfloat16)
    out = jnp.dot(pt, vw, preferred_element_type=jnp.float32) + jnp.dot(
        pp, pv_ref[0], preferred_element_type=jnp.float32)
    o_ref[0] = out.astype(jnp.bfloat16)

def attention(query, keys, values, prompt_key, prompt_value, seg, tok_group, ends, starts, prompt_len, head_dim, parity=0, halves=1, interpret=False):
    tok, cols = query.shape
    heads = cols // head_dim
    block = 256
    window = 1408
    nb = tok // block
    prow = prompt_key.shape[0]
    def by_head(x):
        return x.reshape(x.shape[0], heads, head_dim).transpose(1, 0, 2)
    first = jnp.clip((starts[seg[::block]] // 128) * 128, 0, tok - window).astype(jnp.int32)
    at = first[:, None] + jnp.arange(window, dtype=jnp.int32)[None, :]
    segw = jnp.sum((at[:, :, None] >= ends[None, None, :]).astype(jnp.int32), axis=2).reshape(nb, 1, window)
    segq = seg.reshape(tok, 1)
    grpq = tok_group.reshape(tok, 1)
    kgrp = (jnp.arange(prow, dtype=jnp.int32) // prompt_len).reshape(1, prow)
    first = first[parity::halves]
    segw = segw[parity::halves]
    grid_spec = pltpu.PrefetchScalarGridSpec(
        num_scalar_prefetch=1,
        grid=(heads, nb // halves),
        in_specs=[
            pl.BlockSpec((1, block, head_dim), lambda h, b, fr: (h, halves * b + parity, 0)),
            pl.BlockSpec((1, tok, head_dim), lambda h, b, fr: (h, 0, 0)),
            pl.BlockSpec((1, tok, head_dim), lambda h, b, fr: (h, 0, 0)),
            pl.BlockSpec((1, prow, head_dim), lambda h, b, fr: (h, 0, 0)),
            pl.BlockSpec((1, prow, head_dim), lambda h, b, fr: (h, 0, 0)),
            pl.BlockSpec((block, 1), lambda h, b, fr: (halves * b + parity, 0)),
            pl.BlockSpec((1, 1, window), lambda h, b, fr: (b, 0, 0)),
            pl.BlockSpec((block, 1), lambda h, b, fr: (halves * b + parity, 0)),
            pl.BlockSpec((1, prow), lambda h, b, fr: (0, 0)),
        ],
        out_specs=pl.BlockSpec((1, block, head_dim), lambda h, b, fr: (h, b, 0)),
    )
    out = pl.pallas_call(
        functools.partial(attention_kernel, window=window),
        grid_spec=grid_spec,
        out_shape=jax.ShapeDtypeStruct((heads, tok // halves, head_dim), jnp.bfloat16),
        interpret=interpret,
    )(first, by_head(query), by_head(keys), by_head(values), by_head(prompt_key), by_head(prompt_value), segq, segw, grpq, kgrp)
    return out.transpose(1, 0, 2).reshape(tok // halves, cols)

CROSS = [(0, 2), (2, 0), (1, 3), (3, 1)]
ONCHIP = [(0, 1), (1, 0), (2, 3), (3, 2)]


def gather_tensor(x):
    t = lax.axis_index("tensor")
    upper = t // 2
    core = t % 2
    y = lax.ppermute(x, "tensor", CROSS)
    low = jnp.where(upper == 0, x, y)
    high = jnp.where(upper == 0, y, x)
    pair = jnp.stack([low, high])
    other = lax.ppermute(pair, "tensor", ONCHIP)
    first = core == 0
    return jnp.concatenate(
        [
            jnp.where(first, pair[0], other[0]),
            jnp.where(first, other[0], pair[0]),
            jnp.where(first, pair[1], other[1]),
            jnp.where(first, other[1], pair[1]),
        ],
        axis=0,
    )


def scatter_tensor(part, link_dtype):
    t = lax.axis_index("tensor")
    upper = t // 2
    core = t % 2
    n = part.shape[0] // 4
    blocks = part.reshape((2, 2, n) + part.shape[1:])
    mine = lax.dynamic_index_in_dim(blocks, core, axis=1, keepdims=False)
    theirs = lax.dynamic_index_in_dim(blocks, 1 - core, axis=1, keepdims=False)
    got = lax.ppermute(theirs.astype(link_dtype), "tensor", ONCHIP)
    chip_sum = mine.astype(jnp.float32) + got.astype(jnp.float32)
    keep = lax.dynamic_index_in_dim(chip_sum, upper, axis=0, keepdims=False)
    send = lax.dynamic_index_in_dim(chip_sum, 1 - upper, axis=0, keepdims=False)
    return keep + lax.ppermute(send.astype(link_dtype), "tensor", CROSS).astype(jnp.float32)


def layer_norm(values, gain, bias):
    mean = jnp.mean(values, axis=-1, keepdims=True)
    centred = values - mean
    var = jnp.mean(centred * centred, axis=-1, keepdims=True)
    return centred * lax.rsqrt(var + 1e-05) * gain + bias


def project(block, weight):
    return jnp.dot(block, weight, preferred_element_type=jnp.float32).astype(jnp.bfloat16)


def shards(
    tokens,
    prompts,
    w_attn,
    w_out,
    norm_gain,
    norm_bias,
    w_in,
    b_in,
    w_down,
    index_rows,
    lengths,
    groups,
    candidates,
):
    shard_rows = tokens.shape[0]
    tok_dev = shard_rows * lax.axis_size("tensor")
    columns = w_attn.shape[2]
    heads_here = columns // HEAD_DIM
    scale = HEAD_DIM ** (-0.5)
    whole = lax.all_gather(tokens, "tensor", axis=0, tiled=True)
    query = (jnp.dot(whole, w_attn[0], preferred_element_type=jnp.float32) * scale).astype(
        jnp.bfloat16
    )
    keys = project(whole, w_attn[1])
    values = project(whole, w_attn[2])
    n_dp = lax.axis_size("dp")
    own_prompt = prompts.reshape(-1, prompts.shape[2])
    own_kv = jnp.concatenate([project(own_prompt, w_attn[1]), project(own_prompt, w_attn[2])], axis=1)
    every_kv = lax.all_to_all(
        jnp.broadcast_to(own_kv[None], (n_dp,) + own_kv.shape), "dp", 0, 0, tiled=True
    ).reshape(-1, 2 * columns)
    prompt_key = every_kv[:, :columns]
    prompt_value = every_kv[:, columns:]
    prompt_len = prompts.shape[1]
    prompt_rows = prompt_key.shape[0]
    lens = lengths[0]
    texts_here = lens.shape[0]
    text_ids = jnp.arange(texts_here, dtype=jnp.int32)
    ends = jnp.cumsum(lens)
    position = jnp.arange(tok_dev, dtype=jnp.int32)
    seg = jnp.sum((position[:, None] >= ends[None, :]).astype(jnp.int32), axis=1)
    tok_group = jnp.sum(jnp.where(seg[:, None] == text_ids[None, :], groups[None, :], 0), axis=1)
    starts = ends - lens
    my_start = lax.axis_index("tensor") * shard_rows

    def attend_half(parity):
        context = attention(
            query, keys, values, prompt_key, prompt_value, seg, tok_group, ends, starts, prompt_len,
            HEAD_DIM, parity=parity, halves=2,
        )
        return lax.psum_scatter(
            jnp.dot(context, w_out, preferred_element_type=jnp.float32).astype(jnp.bfloat16),
            "tensor",
            scatter_dimension=0,
            tiled=True,
        ).astype(jnp.float32)

    attn_part = jnp.concatenate([attend_half(0), attend_half(1)], axis=0)
    asked_rows = lax.all_to_all(
        jnp.broadcast_to(candidates[None], (n_dp,) + candidates.shape), "dp", 0, 0, tiled=True
    ).reshape(-1, candidates.shape[1])
    asked_rows, attn_part = lax.optimization_barrier((asked_rows, attn_part))
    normed_rows = layer_norm(
        tokens.astype(jnp.float32) + attn_part, norm_gain[0], norm_bias[0]
    ).astype(jnp.bfloat16)
    half_rows = shard_rows // 2

    def feed_half(rows):
        expanded = jax.nn.gelu(
            jnp.dot(
                gather_tensor(rows),
                w_in,
                preferred_element_type=jnp.float32,
            )
            + b_in,
            approximate=False,
        ).astype(jnp.bfloat16)
        return scatter_tensor(jnp.dot(expanded, w_down, preferred_element_type=jnp.float32), jnp.bfloat16)

    reduced = jnp.concatenate(
        [feed_half(normed_rows[:half_rows]), feed_half(normed_rows[half_rows:])], axis=0
    )
    output = layer_norm(
        normed_rows.astype(jnp.float32) + reduced, norm_gain[1], norm_bias[1]
    ).astype(jnp.bfloat16)
    seg_rows = lax.dynamic_slice_in_dim(seg, my_start, shard_rows, 0)
    member = (text_ids[:, None] == seg_rows[None, :]).astype(jnp.bfloat16)
    partial_sums = jnp.dot(member, output, preferred_element_type=jnp.float32)
    pooled_sums = lax.psum_scatter(partial_sums, "tensor", scatter_dimension=0, tiled=True)
    mine = pooled_sums.shape[0]
    my_lens = lax.dynamic_slice_in_dim(lens, lax.axis_index("tensor") * mine, mine, 0)
    pooled = pooled_sums / my_lens[:, None].astype(jnp.float32)
    square = jnp.mean(pooled * pooled, axis=1, keepdims=True)
    embedding = (pooled * lax.rsqrt(square + 1e-06)).astype(jnp.bfloat16)
    asked_vectors = lax.all_to_all(
        jnp.broadcast_to(embedding[None], (n_dp,) + embedding.shape), "dp", 0, 0, tiled=True
    ).reshape(-1, embedding.shape[1])
    held = index_rows.shape[0]
    local_rows = asked_rows - lax.axis_index("dp") * held
    table = jnp.dot(asked_vectors, index_rows.T, preferred_element_type=jnp.float32) * D ** (-0.5)
    row_ids = jnp.arange(held, dtype=jnp.int32)
    picked = jnp.sum(
        jnp.where(local_rows[:, :, None] == row_ids[None, None, :], table[:, None, :], jnp.float32(0.0)),
        axis=2,
    )
    returned = lax.all_to_all(picked, "dp", 0, 0, tiled=True)
    return jnp.sum(returned.reshape(n_dp, -1, returned.shape[1]), axis=0)


def solution(mesh):
    placed = (
        P(("dp", "tensor"), None),
        P("dp", None, None),
        P(None, None, "tensor"),
        P("tensor", None),
        P(),
        P(),
        P(None, "tensor"),
        P("tensor"),
        P("tensor", None),
        P("dp", None),
        P("dp", None),
        P("dp"),
        P(("dp", "tensor"), None),
    )
    return jax.shard_map(
        shards, mesh=mesh, in_specs=placed, out_specs=P(("dp", "tensor"), None), check_vma=False
    )
```

```python
import jax
import jax.numpy as jnp
from jax import lax
from jax.sharding import PartitionSpec as P
import functools
from jax.experimental import pallas as pl
from jax.experimental.pallas import tpu as pltpu


D = 1024
HEAD_DIM = 64


def attention_kernel(first_ref, q_ref, k_ref, v_ref, pk_ref, pv_ref, segq_ref, segw_ref, grpq_ref, kgrp_ref, o_ref, *, window, head_dim):
    b = pl.program_id(1)
    f = pl.multiple_of(first_ref[b], 128)
    nt = (((1,), (1,)), ((), ()))
    outs = []
    for j in range(q_ref.shape[1] // head_dim):
        lo = j * head_dim
        q = q_ref[:, lo:lo + head_dim]
        kw = k_ref[pl.ds(f, window), lo:lo + head_dim]
        vw = v_ref[pl.ds(f, window), lo:lo + head_dim]
        lt = lax.dot_general(q, kw, nt, preferred_element_type=jnp.float32)
        lt = jnp.where(segq_ref[...] == segw_ref[0], lt, jnp.float32(-1e30))
        lp = lax.dot_general(q, pk_ref[:, lo:lo + head_dim], nt, preferred_element_type=jnp.float32)
        lp = jnp.where(grpq_ref[...] == kgrp_ref[...], lp, jnp.float32(-1e30))
        top = jnp.maximum(jnp.max(lt, axis=1, keepdims=True), jnp.max(lp, axis=1, keepdims=True))
        wt = jnp.exp(lt - top)
        wp = jnp.exp(lp - top)
        total = jnp.sum(wt, axis=1, keepdims=True) + jnp.sum(wp, axis=1, keepdims=True)
        pt = (wt / total).astype(jnp.bfloat16)
        pp = (wp / total).astype(jnp.bfloat16)
        out = jnp.dot(pt, vw, preferred_element_type=jnp.float32) + jnp.dot(
            pp, pv_ref[:, lo:lo + head_dim], preferred_element_type=jnp.float32)
        outs.append(out.astype(jnp.bfloat16))
    o_ref[...] = jnp.concatenate(outs, axis=1)

def attention(query, keys, values, prompt_key, prompt_value, seg, tok_group, ends, starts, prompt_len, head_dim, parity=0, halves=1, interpret=False):
    tok, cols = query.shape
    lanes = 128
    groups = cols // lanes
    block = 256
    window = 1408
    nb = tok // block
    prow = prompt_key.shape[0]
    first = jnp.clip((starts[seg[::block]] // 128) * 128, 0, tok - window).astype(jnp.int32)
    at = first[:, None] + jnp.arange(window, dtype=jnp.int32)[None, :]
    segw = jnp.sum((at[:, :, None] >= ends[None, None, :]).astype(jnp.int32), axis=2).reshape(nb, 1, window)
    segq = seg.reshape(tok, 1)
    grpq = tok_group.reshape(tok, 1)
    kgrp = (jnp.arange(prow, dtype=jnp.int32) // prompt_len).reshape(1, prow)
    first = first[parity::halves]
    segw = segw[parity::halves]
    grid_spec = pltpu.PrefetchScalarGridSpec(
        num_scalar_prefetch=1,
        grid=(groups, nb // halves),
        in_specs=[
            pl.BlockSpec((block, lanes), lambda h, b, fr: (halves * b + parity, h)),
            pl.BlockSpec((tok, lanes), lambda h, b, fr: (0, h)),
            pl.BlockSpec((tok, lanes), lambda h, b, fr: (0, h)),
            pl.BlockSpec((prow, lanes), lambda h, b, fr: (0, h)),
            pl.BlockSpec((prow, lanes), lambda h, b, fr: (0, h)),
            pl.BlockSpec((block, 1), lambda h, b, fr: (halves * b + parity, 0)),
            pl.BlockSpec((1, 1, window), lambda h, b, fr: (b, 0, 0)),
            pl.BlockSpec((block, 1), lambda h, b, fr: (halves * b + parity, 0)),
            pl.BlockSpec((1, prow), lambda h, b, fr: (0, 0)),
        ],
        out_specs=pl.BlockSpec((block, lanes), lambda h, b, fr: (b, h)),
    )
    return pl.pallas_call(
        functools.partial(attention_kernel, window=window, head_dim=head_dim),
        grid_spec=grid_spec,
        out_shape=jax.ShapeDtypeStruct((tok // halves, cols), jnp.bfloat16),
        interpret=interpret,
    )(first, query, keys, values, prompt_key, prompt_value, segq, segw, grpq, kgrp)


CROSS = [(0, 2), (2, 0), (1, 3), (3, 1)]
ONCHIP = [(0, 1), (1, 0), (2, 3), (3, 2)]


def gather_tensor(x):
    t = lax.axis_index("tensor")
    upper = t // 2
    core = t % 2
    y = lax.ppermute(x, "tensor", CROSS)
    low = jnp.where(upper == 0, x, y)
    high = jnp.where(upper == 0, y, x)
    pair = jnp.stack([low, high])
    other = lax.ppermute(pair, "tensor", ONCHIP)
    first = core == 0
    return jnp.concatenate(
        [
            jnp.where(first, pair[0], other[0]),
            jnp.where(first, other[0], pair[0]),
            jnp.where(first, pair[1], other[1]),
            jnp.where(first, other[1], pair[1]),
        ],
        axis=0,
    )


def scatter_tensor(part, link_dtype):
    t = lax.axis_index("tensor")
    upper = t // 2
    core = t % 2
    n = part.shape[0] // 4
    blocks = part.reshape((2, 2, n) + part.shape[1:])
    mine = lax.dynamic_index_in_dim(blocks, core, axis=1, keepdims=False)
    theirs = lax.dynamic_index_in_dim(blocks, 1 - core, axis=1, keepdims=False)
    got = lax.ppermute(theirs.astype(link_dtype), "tensor", ONCHIP)
    chip_sum = mine.astype(jnp.float32) + got.astype(jnp.float32)
    keep = lax.dynamic_index_in_dim(chip_sum, upper, axis=0, keepdims=False)
    send = lax.dynamic_index_in_dim(chip_sum, 1 - upper, axis=0, keepdims=False)
    return keep + lax.ppermute(send.astype(link_dtype), "tensor", CROSS).astype(jnp.float32)


def layer_norm(values, gain, bias):
    mean = jnp.mean(values, axis=-1, keepdims=True)
    centred = values - mean
    var = jnp.mean(centred * centred, axis=-1, keepdims=True)
    return centred * lax.rsqrt(var + 1e-05) * gain + bias


def project(block, weight):
    return jnp.dot(block, weight, preferred_element_type=jnp.float32).astype(jnp.bfloat16)


def shards(
    tokens,
    prompts,
    w_attn,
    w_out,
    norm_gain,
    norm_bias,
    w_in,
    b_in,
    w_down,
    index_rows,
    lengths,
    groups,
    candidates,
):
    shard_rows = tokens.shape[0]
    tok_dev = shard_rows * lax.axis_size("tensor")
    columns = w_attn.shape[2]
    heads_here = columns // HEAD_DIM
    scale = HEAD_DIM ** (-0.5)
    whole = lax.all_gather(tokens, "tensor", axis=0, tiled=True)
    query = (jnp.dot(whole, w_attn[0], preferred_element_type=jnp.float32) * scale).astype(
        jnp.bfloat16
    )
    keys = project(whole, w_attn[1])
    values = project(whole, w_attn[2])
    n_dp = lax.axis_size("dp")
    own_prompt = prompts.reshape(-1, prompts.shape[2])
    own_kv = jnp.concatenate([project(own_prompt, w_attn[1]), project(own_prompt, w_attn[2])], axis=1)
    every_kv = lax.all_to_all(
        jnp.broadcast_to(own_kv[None], (n_dp,) + own_kv.shape), "dp", 0, 0, tiled=True
    ).reshape(-1, 2 * columns)
    prompt_key = every_kv[:, :columns]
    prompt_value = every_kv[:, columns:]
    prompt_len = prompts.shape[1]
    prompt_rows = prompt_key.shape[0]
    lens = lengths[0]
    texts_here = lens.shape[0]
    text_ids = jnp.arange(texts_here, dtype=jnp.int32)
    ends = jnp.cumsum(lens)
    position = jnp.arange(tok_dev, dtype=jnp.int32)
    seg = jnp.sum((position[:, None] >= ends[None, :]).astype(jnp.int32), axis=1)
    tok_group = jnp.sum(jnp.where(seg[:, None] == text_ids[None, :], groups[None, :], 0), axis=1)
    starts = ends - lens
    my_start = lax.axis_index("tensor") * shard_rows

    def attend_half(parity):
        context = attention(
            query, keys, values, prompt_key, prompt_value, seg, tok_group, ends, starts, prompt_len,
            HEAD_DIM, parity=parity, halves=2,
        )
        return lax.psum_scatter(
            jnp.dot(context, w_out, preferred_element_type=jnp.float32).astype(jnp.bfloat16),
            "tensor",
            scatter_dimension=0,
            tiled=True,
        ).astype(jnp.float32)

    attn_part = jnp.concatenate([attend_half(0), attend_half(1)], axis=0)
    asked_rows = lax.all_to_all(
        jnp.broadcast_to(candidates[None], (n_dp,) + candidates.shape), "dp", 0, 0, tiled=True
    ).reshape(-1, candidates.shape[1])
    asked_rows, attn_part = lax.optimization_barrier((asked_rows, attn_part))
    normed_rows = layer_norm(
        tokens.astype(jnp.float32) + attn_part, norm_gain[0], norm_bias[0]
    ).astype(jnp.bfloat16)
    half_rows = shard_rows // 2

    def feed_half(rows):
        expanded = jax.nn.gelu(
            jnp.dot(
                gather_tensor(rows),
                w_in,
                preferred_element_type=jnp.float32,
            )
            + b_in,
            approximate=False,
        ).astype(jnp.bfloat16)
        return scatter_tensor(jnp.dot(expanded, w_down, preferred_element_type=jnp.float32), jnp.bfloat16)

    reduced = jnp.concatenate(
        [feed_half(normed_rows[:half_rows]), feed_half(normed_rows[half_rows:])], axis=0
    )
    output = layer_norm(
        normed_rows.astype(jnp.float32) + reduced, norm_gain[1], norm_bias[1]
    ).astype(jnp.bfloat16)
    seg_rows = lax.dynamic_slice_in_dim(seg, my_start, shard_rows, 0)
    member = (text_ids[:, None] == seg_rows[None, :]).astype(jnp.bfloat16)
    partial_sums = jnp.dot(member, output, preferred_element_type=jnp.float32)
    pooled_sums = lax.psum_scatter(partial_sums, "tensor", scatter_dimension=0, tiled=True)
    mine = pooled_sums.shape[0]
    my_lens = lax.dynamic_slice_in_dim(lens, lax.axis_index("tensor") * mine, mine, 0)
    pooled = pooled_sums / my_lens[:, None].astype(jnp.float32)
    square = jnp.mean(pooled * pooled, axis=1, keepdims=True)
    embedding = (pooled * lax.rsqrt(square + 1e-06)).astype(jnp.bfloat16)
    asked_vectors = lax.all_to_all(
        jnp.broadcast_to(embedding[None], (n_dp,) + embedding.shape), "dp", 0, 0, tiled=True
    ).reshape(-1, embedding.shape[1])
    held = index_rows.shape[0]
    local_rows = asked_rows - lax.axis_index("dp") * held
    table = jnp.dot(asked_vectors, index_rows.T, preferred_element_type=jnp.float32) * D ** (-0.5)
    row_ids = jnp.arange(held, dtype=jnp.int32)
    picked = jnp.sum(
        jnp.where(local_rows[:, :, None] == row_ids[None, None, :], table[:, None, :], jnp.float32(0.0)),
        axis=2,
    )
    returned = lax.all_to_all(picked, "dp", 0, 0, tiled=True)
    return jnp.sum(returned.reshape(n_dp, -1, returned.shape[1]), axis=0)


def solution(mesh):
    placed = (
        P(("dp", "tensor"), None),
        P("dp", None, None),
        P(None, None, "tensor"),
        P("tensor", None),
        P(),
        P(),
        P(None, "tensor"),
        P("tensor"),
        P("tensor", None),
        P("dp", None),
        P("dp", None),
        P("dp"),
        P(("dp", "tensor"), None),
    )
    return jax.shard_map(
        shards, mesh=mesh, in_specs=placed, out_specs=P(("dp", "tensor"), None), check_vma=False
    )
```

```python
import jax
import jax.numpy as jnp
from jax import lax
from jax.sharding import PartitionSpec as P
import functools
from jax.experimental import pallas as pl
from jax.experimental.pallas import tpu as pltpu


D = 1024
HEAD_DIM = 64


def attention_kernel(first_ref, q_ref, k_ref, v_ref, pk_ref, pv_ref, segq_ref, segw_ref, grpq_ref, kgrp_ref, o_ref, *, window, head_dim):
    b = pl.program_id(1)
    f = pl.multiple_of(first_ref[b], 128)
    nt = (((1,), (1,)), ((), ()))
    outs = []
    for j in range(q_ref.shape[1] // head_dim):
        lo = j * head_dim
        q = q_ref[:, lo:lo + head_dim]
        kw = k_ref[pl.ds(f, window), lo:lo + head_dim]
        vw = v_ref[pl.ds(f, window), lo:lo + head_dim]
        lt = lax.dot_general(q, kw, nt, preferred_element_type=jnp.float32)
        lt = jnp.where(segq_ref[...] == segw_ref[0], lt, jnp.float32(-1e30))
        lp = lax.dot_general(q, pk_ref[:, lo:lo + head_dim], nt, preferred_element_type=jnp.float32)
        lp = jnp.where(grpq_ref[...] == kgrp_ref[...], lp, jnp.float32(-1e30))
        top = jnp.maximum(jnp.max(lt, axis=1, keepdims=True), jnp.max(lp, axis=1, keepdims=True))
        wt = jnp.exp(lt - top)
        wp = jnp.exp(lp - top)
        total = jnp.sum(wt, axis=1, keepdims=True) + jnp.sum(wp, axis=1, keepdims=True)
        pt = (wt / total).astype(jnp.bfloat16)
        pp = (wp / total).astype(jnp.bfloat16)
        out = jnp.dot(pt, vw, preferred_element_type=jnp.float32) + jnp.dot(
            pp, pv_ref[:, lo:lo + head_dim], preferred_element_type=jnp.float32)
        outs.append(out.astype(jnp.bfloat16))
    o_ref[...] = jnp.concatenate(outs, axis=1)

def attention(query, keys, values, prompt_key, prompt_value, seg, tok_group, ends, starts, prompt_len, head_dim, parity=0, halves=1, interpret=False):
    tok, cols = query.shape
    lanes = 128
    groups = cols // lanes
    block = 256
    window = 1408
    nb = tok // block
    prow = prompt_key.shape[0]
    first = jnp.clip((starts[seg[::block]] // 128) * 128, 0, tok - window).astype(jnp.int32)
    at = first[:, None] + jnp.arange(window, dtype=jnp.int32)[None, :]
    segw = jnp.sum((at[:, :, None] >= ends[None, None, :]).astype(jnp.int32), axis=2).reshape(nb, 1, window)
    segq = seg.reshape(tok, 1)
    grpq = tok_group.reshape(tok, 1)
    kgrp = (jnp.arange(prow, dtype=jnp.int32) // prompt_len).reshape(1, prow)
    first = first[parity::halves]
    segw = segw[parity::halves]
    grid_spec = pltpu.PrefetchScalarGridSpec(
        num_scalar_prefetch=1,
        grid=(groups, nb // halves),
        in_specs=[
            pl.BlockSpec((block, lanes), lambda h, b, fr: (halves * b + parity, h)),
            pl.BlockSpec((tok, lanes), lambda h, b, fr: (0, h)),
            pl.BlockSpec((tok, lanes), lambda h, b, fr: (0, h)),
            pl.BlockSpec((prow, lanes), lambda h, b, fr: (0, h)),
            pl.BlockSpec((prow, lanes), lambda h, b, fr: (0, h)),
            pl.BlockSpec((block, 1), lambda h, b, fr: (halves * b + parity, 0)),
            pl.BlockSpec((1, 1, window), lambda h, b, fr: (b, 0, 0)),
            pl.BlockSpec((block, 1), lambda h, b, fr: (halves * b + parity, 0)),
            pl.BlockSpec((1, prow), lambda h, b, fr: (0, 0)),
        ],
        out_specs=pl.BlockSpec((block, lanes), lambda h, b, fr: (b, h)),
    )
    return pl.pallas_call(
        functools.partial(attention_kernel, window=window, head_dim=head_dim),
        grid_spec=grid_spec,
        out_shape=jax.ShapeDtypeStruct((tok // halves, cols), jnp.bfloat16),
        interpret=interpret,
    )(first, query, keys, values, prompt_key, prompt_value, segq, segw, grpq, kgrp)


CROSS = [(0, 2), (2, 0), (1, 3), (3, 1)]
ONCHIP = [(0, 1), (1, 0), (2, 3), (3, 2)]


def gather_tensor(x):
    t = lax.axis_index("tensor")
    upper = t // 2
    core = t % 2
    y = lax.ppermute(x, "tensor", CROSS)
    low = jnp.where(upper == 0, x, y)
    high = jnp.where(upper == 0, y, x)
    pair = jnp.stack([low, high])
    other = lax.ppermute(pair, "tensor", ONCHIP)
    first = core == 0
    return jnp.concatenate(
        [
            jnp.where(first, pair[0], other[0]),
            jnp.where(first, other[0], pair[0]),
            jnp.where(first, pair[1], other[1]),
            jnp.where(first, other[1], pair[1]),
        ],
        axis=0,
    )


def scatter_tensor(part, link_dtype):
    t = lax.axis_index("tensor")
    upper = t // 2
    core = t % 2
    n = part.shape[0] // 4
    blocks = part.reshape((2, 2, n) + part.shape[1:])
    mine = lax.dynamic_index_in_dim(blocks, core, axis=1, keepdims=False)
    theirs = lax.dynamic_index_in_dim(blocks, 1 - core, axis=1, keepdims=False)
    got = lax.ppermute(theirs.astype(link_dtype), "tensor", ONCHIP)
    chip_sum = mine.astype(jnp.float32) + got.astype(jnp.float32)
    keep = lax.dynamic_index_in_dim(chip_sum, upper, axis=0, keepdims=False)
    send = lax.dynamic_index_in_dim(chip_sum, 1 - upper, axis=0, keepdims=False)
    return keep + lax.ppermute(send.astype(link_dtype), "tensor", CROSS).astype(jnp.float32)


def feed_forward(rows, w_in, b_in, w_down):
    t = lax.axis_index("tensor")
    upper = t // 2

    def down(block):
        expanded = jax.nn.gelu(
            jnp.dot(block, w_in, preferred_element_type=jnp.float32) + b_in, approximate=False
        ).astype(jnp.bfloat16)
        return jnp.dot(expanded, w_down, preferred_element_type=jnp.float32)

    n = rows.shape[0]
    across = lax.ppermute(rows, "tensor", CROSS)
    own_part = down(rows)
    first = upper == 0
    pair = jnp.stack([jnp.where(first, rows, across), jnp.where(first, across, rows)])
    beside = lax.ppermute(pair, "tensor", ONCHIP)
    across_part = down(across)
    beside_part = down(beside.reshape(2 * n, rows.shape[1])).reshape(2, n, -1)
    got = lax.ppermute(beside_part.astype(jnp.bfloat16), "tensor", ONCHIP)
    mine = jnp.stack([jnp.where(first, own_part, across_part), jnp.where(first, across_part, own_part)])
    chip_sum = mine + got.astype(jnp.float32)
    keep = lax.dynamic_index_in_dim(chip_sum, upper, axis=0, keepdims=False)
    send = lax.dynamic_index_in_dim(chip_sum, 1 - upper, axis=0, keepdims=False)
    return keep + lax.ppermute(send.astype(jnp.bfloat16), "tensor", CROSS).astype(jnp.float32)


def layer_norm(values, gain, bias):
    mean = jnp.mean(values, axis=-1, keepdims=True)
    centred = values - mean
    var = jnp.mean(centred * centred, axis=-1, keepdims=True)
    return centred * lax.rsqrt(var + 1e-05) * gain + bias


def project(block, weight):
    return jnp.dot(block, weight, preferred_element_type=jnp.float32).astype(jnp.bfloat16)


def shards(
    tokens,
    prompts,
    w_attn,
    w_out,
    norm_gain,
    norm_bias,
    w_in,
    b_in,
    w_down,
    index_rows,
    lengths,
    groups,
    candidates,
):
    shard_rows = tokens.shape[0]
    tok_dev = shard_rows * lax.axis_size("tensor")
    columns = w_attn.shape[2]
    heads_here = columns // HEAD_DIM
    scale = HEAD_DIM ** (-0.5)
    whole = lax.all_gather(tokens, "tensor", axis=0, tiled=True)
    query = (jnp.dot(whole, w_attn[0], preferred_element_type=jnp.float32) * scale).astype(
        jnp.bfloat16
    )
    keys = project(whole, w_attn[1])
    values = project(whole, w_attn[2])
    n_dp = lax.axis_size("dp")
    own_prompt = prompts.reshape(-1, prompts.shape[2])
    own_kv = jnp.concatenate([project(own_prompt, w_attn[1]), project(own_prompt, w_attn[2])], axis=1)
    every_kv = lax.all_to_all(
        jnp.broadcast_to(own_kv[None], (n_dp,) + own_kv.shape), "dp", 0, 0, tiled=True
    ).reshape(-1, 2 * columns)
    prompt_key = every_kv[:, :columns]
    prompt_value = every_kv[:, columns:]
    prompt_len = prompts.shape[1]
    prompt_rows = prompt_key.shape[0]
    lens = lengths[0]
    texts_here = lens.shape[0]
    text_ids = jnp.arange(texts_here, dtype=jnp.int32)
    ends = jnp.cumsum(lens)
    position = jnp.arange(tok_dev, dtype=jnp.int32)
    seg = jnp.sum((position[:, None] >= ends[None, :]).astype(jnp.int32), axis=1)
    tok_group = jnp.sum(jnp.where(seg[:, None] == text_ids[None, :], groups[None, :], 0), axis=1)
    starts = ends - lens
    my_start = lax.axis_index("tensor") * shard_rows

    def attend_half(parity):
        context = attention(
            query, keys, values, prompt_key, prompt_value, seg, tok_group, ends, starts, prompt_len,
            HEAD_DIM, parity=parity, halves=2,
        )
        return lax.psum_scatter(
            jnp.dot(context, w_out, preferred_element_type=jnp.float32).astype(jnp.bfloat16),
            "tensor",
            scatter_dimension=0,
            tiled=True,
        ).astype(jnp.float32)

    attn_part = jnp.concatenate([attend_half(0), attend_half(1)], axis=0)
    asked_rows = lax.all_to_all(
        jnp.broadcast_to(candidates[None], (n_dp,) + candidates.shape), "dp", 0, 0, tiled=True
    ).reshape(-1, candidates.shape[1])
    asked_rows, attn_part = lax.optimization_barrier((asked_rows, attn_part))
    normed_rows = layer_norm(
        tokens.astype(jnp.float32) + attn_part, norm_gain[0], norm_bias[0]
    ).astype(jnp.bfloat16)
    reduced = feed_forward(normed_rows, w_in, b_in, w_down)
    output = layer_norm(
        normed_rows.astype(jnp.float32) + reduced, norm_gain[1], norm_bias[1]
    ).astype(jnp.bfloat16)
    seg_rows = lax.dynamic_slice_in_dim(seg, my_start, shard_rows, 0)
    member = (text_ids[:, None] == seg_rows[None, :]).astype(jnp.bfloat16)
    partial_sums = jnp.dot(member, output, preferred_element_type=jnp.float32)
    pooled_sums = lax.psum_scatter(partial_sums, "tensor", scatter_dimension=0, tiled=True)
    mine = pooled_sums.shape[0]
    my_lens = lax.dynamic_slice_in_dim(lens, lax.axis_index("tensor") * mine, mine, 0)
    pooled = pooled_sums / my_lens[:, None].astype(jnp.float32)
    square = jnp.mean(pooled * pooled, axis=1, keepdims=True)
    embedding = (pooled * lax.rsqrt(square + 1e-06)).astype(jnp.bfloat16)
    asked_vectors = lax.all_to_all(
        jnp.broadcast_to(embedding[None], (n_dp,) + embedding.shape), "dp", 0, 0, tiled=True
    ).reshape(-1, embedding.shape[1])
    held = index_rows.shape[0]
    local_rows = asked_rows - lax.axis_index("dp") * held
    table = jnp.dot(asked_vectors, index_rows.T, preferred_element_type=jnp.float32) * D ** (-0.5)
    row_ids = jnp.arange(held, dtype=jnp.int32)
    picked = jnp.sum(
        jnp.where(local_rows[:, :, None] == row_ids[None, None, :], table[:, None, :], jnp.float32(0.0)),
        axis=2,
    )
    returned = lax.all_to_all(picked, "dp", 0, 0, tiled=True)
    return jnp.sum(returned.reshape(n_dp, -1, returned.shape[1]), axis=0)


def solution(mesh):
    placed = (
        P(("dp", "tensor"), None),
        P("dp", None, None),
        P(None, None, "tensor"),
        P("tensor", None),
        P(),
        P(),
        P(None, "tensor"),
        P("tensor"),
        P("tensor", None),
        P("dp", None),
        P("dp", None),
        P("dp"),
        P(("dp", "tensor"), None),
    )
    return jax.shard_map(
        shards, mesh=mesh, in_specs=placed, out_specs=P(("dp", "tensor"), None), check_vma=False
    )
```

```python
import jax
import jax.numpy as jnp
from jax import lax
from jax.sharding import PartitionSpec as P
import functools
from jax.experimental import pallas as pl
from jax.experimental.pallas import tpu as pltpu


D = 1024
HEAD_DIM = 64


def attention_kernel(first_ref, q_ref, k_ref, v_ref, pk_ref, pv_ref, segq_ref, segw_ref, grpq_ref, kgrp_ref, o_ref, *, window, head_dim):
    b = pl.program_id(1)
    f = pl.multiple_of(first_ref[b], 128)
    nt = (((1,), (1,)), ((), ()))
    outs = []
    for j in range(q_ref.shape[1] // head_dim):
        lo = j * head_dim
        q = q_ref[:, lo:lo + head_dim]
        kw = k_ref[pl.ds(f, window), lo:lo + head_dim]
        vw = v_ref[pl.ds(f, window), lo:lo + head_dim]
        lt = lax.dot_general(q, kw, nt, preferred_element_type=jnp.float32)
        lt = jnp.where(segq_ref[...] == segw_ref[0], lt, jnp.float32(-1e30))
        lp = lax.dot_general(q, pk_ref[:, lo:lo + head_dim], nt, preferred_element_type=jnp.float32)
        lp = jnp.where(grpq_ref[...] == kgrp_ref[...], lp, jnp.float32(-1e30))
        top = jnp.maximum(jnp.max(lt, axis=1, keepdims=True), jnp.max(lp, axis=1, keepdims=True))
        wt = jnp.exp(lt - top)
        wp = jnp.exp(lp - top)
        total = jnp.sum(wt, axis=1, keepdims=True) + jnp.sum(wp, axis=1, keepdims=True)
        pt = (wt / total).astype(jnp.bfloat16)
        pp = (wp / total).astype(jnp.bfloat16)
        out = jnp.dot(pt, vw, preferred_element_type=jnp.float32) + jnp.dot(
            pp, pv_ref[:, lo:lo + head_dim], preferred_element_type=jnp.float32)
        outs.append(out.astype(jnp.bfloat16))
    o_ref[...] = jnp.concatenate(outs, axis=1)

def attention(query, keys, values, prompt_key, prompt_value, seg, tok_group, ends, starts, prompt_len, head_dim, parity=0, halves=1, interpret=False):
    tok, cols = query.shape
    lanes = 128
    groups = cols // lanes
    block = 256
    window = 1408
    nb = tok // block
    prow = prompt_key.shape[0]
    first = jnp.clip((starts[seg[::block]] // 128) * 128, 0, tok - window).astype(jnp.int32)
    at = first[:, None] + jnp.arange(window, dtype=jnp.int32)[None, :]
    segw = jnp.sum((at[:, :, None] >= ends[None, None, :]).astype(jnp.int32), axis=2).reshape(nb, 1, window)
    segq = seg.reshape(tok, 1)
    grpq = tok_group.reshape(tok, 1)
    kgrp = (jnp.arange(prow, dtype=jnp.int32) // prompt_len).reshape(1, prow)
    first = first[parity::halves]
    segw = segw[parity::halves]
    grid_spec = pltpu.PrefetchScalarGridSpec(
        num_scalar_prefetch=1,
        grid=(groups, nb // halves),
        in_specs=[
            pl.BlockSpec((block, lanes), lambda h, b, fr: (halves * b + parity, h)),
            pl.BlockSpec((tok, lanes), lambda h, b, fr: (0, h)),
            pl.BlockSpec((tok, lanes), lambda h, b, fr: (0, h)),
            pl.BlockSpec((prow, lanes), lambda h, b, fr: (0, h)),
            pl.BlockSpec((prow, lanes), lambda h, b, fr: (0, h)),
            pl.BlockSpec((block, 1), lambda h, b, fr: (halves * b + parity, 0)),
            pl.BlockSpec((1, 1, window), lambda h, b, fr: (b, 0, 0)),
            pl.BlockSpec((block, 1), lambda h, b, fr: (halves * b + parity, 0)),
            pl.BlockSpec((1, prow), lambda h, b, fr: (0, 0)),
        ],
        out_specs=pl.BlockSpec((block, lanes), lambda h, b, fr: (b, h)),
    )
    return pl.pallas_call(
        functools.partial(attention_kernel, window=window, head_dim=head_dim),
        grid_spec=grid_spec,
        out_shape=jax.ShapeDtypeStruct((tok // halves, cols), jnp.bfloat16),
        interpret=interpret,
    )(first, query, keys, values, prompt_key, prompt_value, segq, segw, grpq, kgrp)


CROSS = [(0, 2), (2, 0), (1, 3), (3, 1)]
ONCHIP = [(0, 1), (1, 0), (2, 3), (3, 2)]


def gather_tensor(x):
    t = lax.axis_index("tensor")
    upper = t // 2
    core = t % 2
    y = lax.ppermute(x, "tensor", CROSS)
    low = jnp.where(upper == 0, x, y)
    high = jnp.where(upper == 0, y, x)
    pair = jnp.stack([low, high])
    other = lax.ppermute(pair, "tensor", ONCHIP)
    first = core == 0
    return jnp.concatenate(
        [
            jnp.where(first, pair[0], other[0]),
            jnp.where(first, other[0], pair[0]),
            jnp.where(first, pair[1], other[1]),
            jnp.where(first, other[1], pair[1]),
        ],
        axis=0,
    )


def scatter_tensor(part, link_dtype):
    t = lax.axis_index("tensor")
    upper = t // 2
    core = t % 2
    n = part.shape[0] // 4
    blocks = part.reshape((2, 2, n) + part.shape[1:])
    mine = lax.dynamic_index_in_dim(blocks, core, axis=1, keepdims=False)
    theirs = lax.dynamic_index_in_dim(blocks, 1 - core, axis=1, keepdims=False)
    got = lax.ppermute(theirs.astype(link_dtype), "tensor", ONCHIP)
    chip_sum = mine.astype(jnp.float32) + got.astype(jnp.float32)
    keep = lax.dynamic_index_in_dim(chip_sum, upper, axis=0, keepdims=False)
    send = lax.dynamic_index_in_dim(chip_sum, 1 - upper, axis=0, keepdims=False)
    return keep + lax.ppermute(send.astype(link_dtype), "tensor", CROSS).astype(jnp.float32)


def feed_forward(rows, w_in, b_in, w_down):
    t = lax.axis_index("tensor")
    upper = t // 2

    def down(block):
        expanded = jax.nn.gelu(
            jnp.dot(block, w_in, preferred_element_type=jnp.float32) + b_in, approximate=False
        ).astype(jnp.bfloat16)
        return jnp.dot(expanded, w_down, preferred_element_type=jnp.float32)

    n = rows.shape[0]
    across = lax.ppermute(rows, "tensor", CROSS)
    own_part = down(rows)
    first = upper == 0
    pair = jnp.stack([jnp.where(first, rows, across), jnp.where(first, across, rows)])
    beside = lax.ppermute(pair, "tensor", ONCHIP)
    across_part = down(across)
    beside_part = down(beside.reshape(2 * n, rows.shape[1])).reshape(2, n, -1)
    got = lax.ppermute(beside_part.astype(jnp.bfloat16), "tensor", ONCHIP)
    mine = jnp.stack([jnp.where(first, own_part, across_part), jnp.where(first, across_part, own_part)])
    chip_sum = mine + got.astype(jnp.float32)
    keep = lax.dynamic_index_in_dim(chip_sum, upper, axis=0, keepdims=False)
    send = lax.dynamic_index_in_dim(chip_sum, 1 - upper, axis=0, keepdims=False)
    return keep + lax.ppermute(send.astype(jnp.bfloat16), "tensor", CROSS).astype(jnp.float32)


def layer_norm(values, gain, bias):
    mean = jnp.mean(values, axis=-1, keepdims=True)
    centred = values - mean
    var = jnp.mean(centred * centred, axis=-1, keepdims=True)
    return centred * lax.rsqrt(var + 1e-05) * gain + bias


def project(block, weight):
    return jnp.dot(block, weight, preferred_element_type=jnp.float32).astype(jnp.bfloat16)


def shards(
    tokens,
    prompts,
    w_attn,
    w_out,
    norm_gain,
    norm_bias,
    w_in,
    b_in,
    w_down,
    index_rows,
    lengths,
    groups,
    candidates,
):
    shard_rows = tokens.shape[0]
    tok_dev = shard_rows * lax.axis_size("tensor")
    columns = w_attn.shape[2]
    heads_here = columns // HEAD_DIM
    scale = HEAD_DIM ** (-0.5)
    whole = lax.all_gather(tokens, "tensor", axis=0, tiled=True)
    query = (jnp.dot(whole, w_attn[0], preferred_element_type=jnp.float32) * scale).astype(
        jnp.bfloat16
    )
    keys = project(whole, w_attn[1])
    values = project(whole, w_attn[2])
    n_dp = lax.axis_size("dp")
    own_prompt = prompts.reshape(-1, prompts.shape[2])
    own_kv = jnp.concatenate([project(own_prompt, w_attn[1]), project(own_prompt, w_attn[2])], axis=1)
    every_kv = lax.all_to_all(
        jnp.broadcast_to(own_kv[None], (n_dp,) + own_kv.shape), "dp", 0, 0, tiled=True
    ).reshape(-1, 2 * columns)
    prompt_key = every_kv[:, :columns]
    prompt_value = every_kv[:, columns:]
    prompt_len = prompts.shape[1]
    prompt_rows = prompt_key.shape[0]
    lens = lengths[0]
    texts_here = lens.shape[0]
    text_ids = jnp.arange(texts_here, dtype=jnp.int32)
    ends = jnp.cumsum(lens)
    position = jnp.arange(tok_dev, dtype=jnp.int32)
    seg = jnp.sum((position[:, None] >= ends[None, :]).astype(jnp.int32), axis=1)
    tok_group = jnp.sum(jnp.where(seg[:, None] == text_ids[None, :], groups[None, :], 0), axis=1)
    starts = ends - lens
    my_start = lax.axis_index("tensor") * shard_rows

    def attend_half(parity):
        context = attention(
            query, keys, values, prompt_key, prompt_value, seg, tok_group, ends, starts, prompt_len,
            HEAD_DIM, parity=parity, halves=2,
        )
        return lax.psum_scatter(
            jnp.dot(context, w_out, preferred_element_type=jnp.float32).astype(jnp.bfloat16),
            "tensor",
            scatter_dimension=0,
            tiled=True,
        ).astype(jnp.float32)

    attn_part = jnp.concatenate([attend_half(0), attend_half(1)], axis=0)
    normed_rows = layer_norm(
        tokens.astype(jnp.float32) + attn_part, norm_gain[0], norm_bias[0]
    ).astype(jnp.bfloat16)
    asked, normed_rows = lax.optimization_barrier((candidates, normed_rows))
    asked_rows = lax.all_to_all(
        jnp.broadcast_to(asked[None], (n_dp,) + asked.shape), "dp", 0, 0, tiled=True
    ).reshape(-1, asked.shape[1])
    reduced = feed_forward(normed_rows, w_in, b_in, w_down)
    output = layer_norm(
        normed_rows.astype(jnp.float32) + reduced, norm_gain[1], norm_bias[1]
    ).astype(jnp.bfloat16)
    seg_rows = lax.dynamic_slice_in_dim(seg, my_start, shard_rows, 0)
    member = (text_ids[:, None] == seg_rows[None, :]).astype(jnp.bfloat16)
    partial_sums = jnp.dot(member, output, preferred_element_type=jnp.float32)
    pooled_sums = lax.psum_scatter(partial_sums, "tensor", scatter_dimension=0, tiled=True)
    mine = pooled_sums.shape[0]
    my_lens = lax.dynamic_slice_in_dim(lens, lax.axis_index("tensor") * mine, mine, 0)
    pooled = pooled_sums / my_lens[:, None].astype(jnp.float32)
    square = jnp.mean(pooled * pooled, axis=1, keepdims=True)
    embedding = (pooled * lax.rsqrt(square + 1e-06)).astype(jnp.bfloat16)
    asked_vectors = lax.all_to_all(
        jnp.broadcast_to(embedding[None], (n_dp,) + embedding.shape), "dp", 0, 0, tiled=True
    ).reshape(-1, embedding.shape[1])
    held = index_rows.shape[0]
    local_rows = asked_rows - lax.axis_index("dp") * held
    table = jnp.dot(asked_vectors, index_rows.T, preferred_element_type=jnp.float32) * D ** (-0.5)
    row_ids = jnp.arange(held, dtype=jnp.int32)
    picked = jnp.sum(
        jnp.where(local_rows[:, :, None] == row_ids[None, None, :], table[:, None, :], jnp.float32(0.0)),
        axis=2,
    )
    returned = lax.all_to_all(picked, "dp", 0, 0, tiled=True)
    return jnp.sum(returned.reshape(n_dp, -1, returned.shape[1]), axis=0)


def solution(mesh):
    placed = (
        P(("dp", "tensor"), None),
        P("dp", None, None),
        P(None, None, "tensor"),
        P("tensor", None),
        P(),
        P(),
        P(None, "tensor"),
        P("tensor"),
        P("tensor", None),
        P("dp", None),
        P("dp", None),
        P("dp"),
        P(("dp", "tensor"), None),
    )
    return jax.shard_map(
        shards, mesh=mesh, in_specs=placed, out_specs=P(("dp", "tensor"), None), check_vma=False
    )
```

```python
import jax
import jax.numpy as jnp
from jax import lax
from jax.sharding import PartitionSpec as P
import functools
from jax.experimental import pallas as pl
from jax.experimental.pallas import tpu as pltpu


D = 1024
HEAD_DIM = 64


def attention_kernel(first_ref, q_ref, k_ref, v_ref, pk_ref, pv_ref, segq_ref, segw_ref, grpq_ref, kgrp_ref, o_ref, *, window, head_dim):
    b = pl.program_id(1)
    f = pl.multiple_of(first_ref[b], 128)
    nt = (((1,), (1,)), ((), ()))
    outs = []
    for j in range(q_ref.shape[1] // head_dim):
        lo = j * head_dim
        q = q_ref[:, lo:lo + head_dim]
        kw = k_ref[pl.ds(f, window), lo:lo + head_dim]
        vw = v_ref[pl.ds(f, window), lo:lo + head_dim]
        lt = lax.dot_general(q, kw, nt, preferred_element_type=jnp.float32)
        lt = jnp.where(segq_ref[...] == segw_ref[0], lt, jnp.float32(-1e30))
        lp = lax.dot_general(q, pk_ref[:, lo:lo + head_dim], nt, preferred_element_type=jnp.float32)
        lp = jnp.where(grpq_ref[...] == kgrp_ref[...], lp, jnp.float32(-1e30))
        top = jnp.maximum(jnp.max(lt, axis=1, keepdims=True), jnp.max(lp, axis=1, keepdims=True))
        wt = jnp.exp(lt - top)
        wp = jnp.exp(lp - top)
        total = jnp.sum(wt, axis=1, keepdims=True) + jnp.sum(wp, axis=1, keepdims=True)
        pt = (wt / total).astype(jnp.bfloat16)
        pp = (wp / total).astype(jnp.bfloat16)
        out = jnp.dot(pt, vw, preferred_element_type=jnp.float32) + jnp.dot(
            pp, pv_ref[:, lo:lo + head_dim], preferred_element_type=jnp.float32)
        outs.append(out.astype(jnp.bfloat16))
    o_ref[...] = jnp.concatenate(outs, axis=1)


def attention(query, keys, values, prompt_key, prompt_value, seg, tok_group, ends, starts, prompt_len, head_dim, parity=0, halves=1, interpret=False):
    tok, cols = query.shape
    lanes = 128
    groups = cols // lanes
    block = 256
    window = 1408
    nb = tok // block
    prow = prompt_key.shape[0]
    first = jnp.clip((starts[seg[::block]] // 128) * 128, 0, tok - window).astype(jnp.int32)
    at = first[:, None] + jnp.arange(window, dtype=jnp.int32)[None, :]
    segw = jnp.sum((at[:, :, None] >= ends[None, None, :]).astype(jnp.int32), axis=2).reshape(nb, 1, window)
    segq = seg.reshape(tok, 1)
    grpq = tok_group.reshape(tok, 1)
    kgrp = (jnp.arange(prow, dtype=jnp.int32) // prompt_len).reshape(1, prow)
    first = first[parity::halves]
    segw = segw[parity::halves]
    grid_spec = pltpu.PrefetchScalarGridSpec(
        num_scalar_prefetch=1,
        grid=(groups, nb // halves),
        in_specs=[
            pl.BlockSpec((block, lanes), lambda h, b, fr: (halves * b + parity, h)),
            pl.BlockSpec((tok, lanes), lambda h, b, fr: (0, h)),
            pl.BlockSpec((tok, lanes), lambda h, b, fr: (0, h)),
            pl.BlockSpec((prow, lanes), lambda h, b, fr: (0, h)),
            pl.BlockSpec((prow, lanes), lambda h, b, fr: (0, h)),
            pl.BlockSpec((block, 1), lambda h, b, fr: (halves * b + parity, 0)),
            pl.BlockSpec((1, 1, window), lambda h, b, fr: (b, 0, 0)),
            pl.BlockSpec((block, 1), lambda h, b, fr: (halves * b + parity, 0)),
            pl.BlockSpec((1, prow), lambda h, b, fr: (0, 0)),
        ],
        out_specs=pl.BlockSpec((block, lanes), lambda h, b, fr: (b, h)),
    )
    return pl.pallas_call(
        functools.partial(attention_kernel, window=window, head_dim=head_dim),
        grid_spec=grid_spec,
        out_shape=jax.ShapeDtypeStruct((tok // halves, cols), jnp.bfloat16),
        interpret=interpret,
    )(first, query, keys, values, prompt_key, prompt_value, segq, segw, grpq, kgrp)


CROSS = [(0, 2), (2, 0), (1, 3), (3, 1)]
ONCHIP = [(0, 1), (1, 0), (2, 3), (3, 2)]


def feed_forward(rows, w_in, b_in, w_down):
    t = lax.axis_index("tensor")
    upper = t // 2

    def down(block):
        expanded = jax.nn.gelu(
            jnp.dot(block, w_in, preferred_element_type=jnp.float32) + b_in, approximate=False
        ).astype(jnp.bfloat16)
        return jnp.dot(expanded, w_down, preferred_element_type=jnp.float32)

    n = rows.shape[0]
    across = lax.ppermute(rows, "tensor", CROSS)
    own_part = down(rows)
    across, own_part = lax.optimization_barrier((across, own_part))
    first = upper == 0
    pair = jnp.stack([jnp.where(first, rows, across), jnp.where(first, across, rows)])
    beside = lax.ppermute(pair, "tensor", ONCHIP)
    across_part = down(across)
    beside_part = down(beside.reshape(2 * n, rows.shape[1])).reshape(2, n, -1)
    got = lax.ppermute(beside_part.astype(jnp.bfloat16), "tensor", ONCHIP)
    mine = jnp.stack([jnp.where(first, own_part, across_part), jnp.where(first, across_part, own_part)])
    chip_sum = mine + got.astype(jnp.float32)
    keep = lax.dynamic_index_in_dim(chip_sum, upper, axis=0, keepdims=False)
    send = lax.dynamic_index_in_dim(chip_sum, 1 - upper, axis=0, keepdims=False)
    return keep + lax.ppermute(send.astype(jnp.bfloat16), "tensor", CROSS).astype(jnp.float32)


def layer_norm(values, gain, bias):
    mean = jnp.mean(values, axis=-1, keepdims=True)
    centred = values - mean
    var = jnp.mean(centred * centred, axis=-1, keepdims=True)
    return centred * lax.rsqrt(var + 1e-05) * gain + bias


def project(block, weight):
    return jnp.dot(block, weight, preferred_element_type=jnp.float32).astype(jnp.bfloat16)


def shards(
    tokens,
    prompts,
    w_attn,
    w_out,
    norm_gain,
    norm_bias,
    w_in,
    b_in,
    w_down,
    index_rows,
    lengths,
    groups,
    candidates,
):
    shard_rows = tokens.shape[0]
    tok_dev = shard_rows * lax.axis_size("tensor")
    columns = w_attn.shape[2]
    scale = HEAD_DIM ** (-0.5)
    whole = lax.all_gather(tokens, "tensor", axis=0, tiled=True)
    query = (jnp.dot(whole, w_attn[0], preferred_element_type=jnp.float32) * scale).astype(
        jnp.bfloat16
    )
    keys = project(whole, w_attn[1])
    values = project(whole, w_attn[2])
    n_dp = lax.axis_size("dp")
    own_prompt = prompts.reshape(-1, prompts.shape[2])
    own_kv = jnp.concatenate([project(own_prompt, w_attn[1]), project(own_prompt, w_attn[2])], axis=1)
    every_kv = lax.all_to_all(
        jnp.broadcast_to(own_kv[None], (n_dp,) + own_kv.shape), "dp", 0, 0, tiled=True
    ).reshape(-1, 2 * columns)
    prompt_key = every_kv[:, :columns]
    prompt_value = every_kv[:, columns:]
    prompt_len = prompts.shape[1]
    lens = lengths[0]
    texts_here = lens.shape[0]
    text_ids = jnp.arange(texts_here, dtype=jnp.int32)
    ends = jnp.cumsum(lens)
    position = jnp.arange(tok_dev, dtype=jnp.int32)
    seg = jnp.sum((position[:, None] >= ends[None, :]).astype(jnp.int32), axis=1)
    tok_group = jnp.sum(jnp.where(seg[:, None] == text_ids[None, :], groups[None, :], 0), axis=1)
    starts = ends - lens
    my_start = lax.axis_index("tensor") * shard_rows

    def attend_half(parity):
        context = attention(
            query, keys, values, prompt_key, prompt_value, seg, tok_group, ends, starts, prompt_len,
            HEAD_DIM, parity=parity, halves=2,
        )
        return lax.psum_scatter(
            jnp.dot(context, w_out, preferred_element_type=jnp.float32).astype(jnp.bfloat16),
            "tensor",
            scatter_dimension=0,
            tiled=True,
        ).astype(jnp.float32)

    attn_part = jnp.concatenate([attend_half(0), attend_half(1)], axis=0)
    normed_rows = layer_norm(
        tokens.astype(jnp.float32) + attn_part, norm_gain[0], norm_bias[0]
    ).astype(jnp.bfloat16)
    asked, normed_rows = lax.optimization_barrier((candidates, normed_rows))
    asked_rows = lax.all_to_all(
        jnp.broadcast_to(asked[None], (n_dp,) + asked.shape), "dp", 0, 0, tiled=True
    ).reshape(-1, asked.shape[1])
    reduced = feed_forward(normed_rows, w_in, b_in, w_down)
    output = layer_norm(
        normed_rows.astype(jnp.float32) + reduced, norm_gain[1], norm_bias[1]
    ).astype(jnp.bfloat16)
    seg_rows = lax.dynamic_slice_in_dim(seg, my_start, shard_rows, 0)
    member = (text_ids[:, None] == seg_rows[None, :]).astype(jnp.bfloat16)
    partial_sums = jnp.dot(member, output, preferred_element_type=jnp.float32)
    pooled_sums = lax.psum_scatter(partial_sums, "tensor", scatter_dimension=0, tiled=True)
    mine = pooled_sums.shape[0]
    my_lens = lax.dynamic_slice_in_dim(lens, lax.axis_index("tensor") * mine, mine, 0)
    pooled = pooled_sums / my_lens[:, None].astype(jnp.float32)
    square = jnp.mean(pooled * pooled, axis=1, keepdims=True)
    embedding = (pooled * lax.rsqrt(square + 1e-06)).astype(jnp.bfloat16)
    asked_vectors = lax.all_to_all(
        jnp.broadcast_to(embedding[None], (n_dp,) + embedding.shape), "dp", 0, 0, tiled=True
    ).reshape(-1, embedding.shape[1])
    held = index_rows.shape[0]
    local_rows = asked_rows - lax.axis_index("dp") * held
    table = jnp.dot(asked_vectors, index_rows.T, preferred_element_type=jnp.float32) * D ** (-0.5)
    row_ids = jnp.arange(held, dtype=jnp.int32)
    picked = jnp.sum(
        jnp.where(local_rows[:, :, None] == row_ids[None, None, :], table[:, None, :], jnp.float32(0.0)),
        axis=2,
    )
    returned = lax.all_to_all(picked, "dp", 0, 0, tiled=True)
    return jnp.sum(returned.reshape(n_dp, -1, returned.shape[1]), axis=0)


def solution(mesh):
    placed = (
        P(("dp", "tensor"), None),
        P("dp", None, None),
        P(None, None, "tensor"),
        P("tensor", None),
        P(),
        P(),
        P(None, "tensor"),
        P("tensor"),
        P("tensor", None),
        P("dp", None),
        P("dp", None),
        P("dp"),
        P(("dp", "tensor"), None),
    )
    return jax.shard_map(
        shards, mesh=mesh, in_specs=placed, out_specs=P(("dp", "tensor"), None), check_vma=False
    )
```
